512 devices in a mesh: req: 64 (over z, x_lo, core), tp: 8 (over x_hi, y).
Axes of the slice: x: 4 (x_hi: 2, x_lo: 2; x = x_hi * 2 + x_lo), y: 4, z: 16, core: 2. Of those that a mesh axis runs over, the one named last changes fastest.
Arguments:
- queries: bfloat16 [8192, 8192], P('req', 'tp'), may hold values from -16 to 16
- span_rotated_keys: bfloat16 [8192, 1024], P('req', 'tp'), may hold values from -6 to 6
- span_token_values: bfloat16 [8192, 1024], P('req', 'tp'), may hold values from -6 to 6
- cache_keys: bfloat16 [65536, 1024], P('req', 'tp'), may hold values from -6 to 6
- prompt_cache_values: bfloat16 [65536, 1024], P('req', 'tp'), may hold values from -6 to 6
- lengths: int32 [8], replicated, may hold values from 2 to 8192, as said below
Outputs:
- attention: bfloat16 [8192, 8192], P(('req', 'tp'))
The draws below stay inside these ranges and needn't reach their ends.
Inputs may be any that keep to these rules, and one draw needn't show every extreme that they name: `lengths`: each group's cached prompt length; one group's is exactly 8192.
All inputs are finite; a program needn't handle non-finite values.
Results may differ from the reference program's by a relative error of at most 0.0045.
Values may be sent and summed in bfloat16 or wider, within the bound.
No kernel may reach another device: no remote copies, remote signals or barrier semaphores. Data moves between devices by JAX's collectives and lax.ppermute only.
A program may use at most 64 MiB of HBM per device.

```python
import math
import jax
import jax.numpy as jnp
from jax import lax

QUERY_HEADS = 64
KEY_VALUE_HEADS = 8
HEAD_SIZE = 128
SPAN_TOKENS = 1024
REQUEST_GROUPS = 8
ALL_SPAN_TOKENS = 8192
MAX_PROMPT_ROWS = 8192


def draw_queries(key, part):
    value_rows_joined = jnp.clip(jax.random.normal(jax.random.fold_in(key, 1), (ALL_SPAN_TOKENS, QUERY_HEADS * HEAD_SIZE), jnp.float32) * 3.5, -16.0, 16.0)
    return value_rows_joined.astype(jnp.bfloat16)


def draw_cache_keys(key, part):
    value_rows_joined = jnp.clip(jax.random.normal(jax.random.fold_in(key, 2), (REQUEST_GROUPS * MAX_PROMPT_ROWS, KEY_VALUE_HEADS * HEAD_SIZE), jnp.float32), -6.0, 6.0)
    return value_rows_joined.astype(jnp.bfloat16)


def draw_lengths(key, part):
    drawn = jax.random.randint(jax.random.fold_in(key, 3), (REQUEST_GROUPS,), 2, MAX_PROMPT_ROWS + 1, dtype=jnp.int32)
    longest = jax.random.randint(jax.random.fold_in(key, 4), (), 0, REQUEST_GROUPS, dtype=jnp.int32)
    return jnp.where(jnp.arange(REQUEST_GROUPS, dtype=jnp.int32) == longest, MAX_PROMPT_ROWS, drawn).astype(jnp.int32)


def steps_of(rng, extent, cuts, least, top_value):
    def one(dim, shards_of):
        draws = jax.random.uniform(jax.random.fold_in(jax.random.fold_in(rng, 6), dim), (shards_of,), jnp.float32, least / len(cuts), top_value / len(cuts))
        return jnp.repeat(jnp.exp(draws), extent[dim] // shards_of).reshape((-1,) + (1,) * (len(extent) - dim - 1))

    level = one(*cuts[0])
    for cut in cuts[1:]:
        level = level * one(*cut)
    return level


def noise(rng, dims, scale, reach, shards=(), kind=jnp.bfloat16):
    entries = scale * jax.random.normal(rng, dims, jnp.float32)
    if shards:
        entries = entries * steps_of(rng, dims, shards, -0.22, 0.18)
    return jnp.clip(entries, -reach, reach).astype(kind)


def setup_inputs(seed: int = 0) -> dict:
    splits = jax.random.split(jax.random.key(seed), 7)
    return {
        "queries": draw_queries(jax.random.fold_in(splits[6], 71), 0),
        "span_rotated_keys": noise(splits[1], (ALL_SPAN_TOKENS, KEY_VALUE_HEADS * HEAD_SIZE), 1.0, 6.0, ((0, 64), (1, 8))),
        "span_token_values": noise(splits[2], (ALL_SPAN_TOKENS, KEY_VALUE_HEADS * HEAD_SIZE), 1.0, 6.0, ((0, 64), (1, 8))),
        "cache_keys": draw_cache_keys(jax.random.fold_in(splits[6], 71), 0),
        "prompt_cache_values": noise(splits[4], (REQUEST_GROUPS * MAX_PROMPT_ROWS, KEY_VALUE_HEADS * HEAD_SIZE), 1.0, 6.0, ((0, 64), (1, 8))),
        "lengths": draw_lengths(jax.random.fold_in(splits[6], 71), 0),
    }


NEG_FILL = -1e+30

def reference(queries, span_rotated_keys, span_token_values, cache_keys, prompt_cache_values, lengths):
    heads_per_group = QUERY_HEADS // KEY_VALUE_HEADS
    score_scale = 1.0 / math.sqrt(HEAD_SIZE)
    query_head_rows = queries.reshape(REQUEST_GROUPS, SPAN_TOKENS, KEY_VALUE_HEADS, heads_per_group, HEAD_SIZE).transpose(0, 2, 3, 1, 4)
    query_head_rows = query_head_rows.reshape(REQUEST_GROUPS * KEY_VALUE_HEADS * heads_per_group, SPAN_TOKENS, HEAD_SIZE)

    def key_layout(cached_rows, span_portion):
        joined_rows = jnp.concatenate([cached_rows.reshape(REQUEST_GROUPS, MAX_PROMPT_ROWS, KEY_VALUE_HEADS, HEAD_SIZE), span_portion.reshape(REQUEST_GROUPS, SPAN_TOKENS, KEY_VALUE_HEADS, HEAD_SIZE)], axis=1)
        return joined_rows.transpose(0, 2, 1, 3).reshape(REQUEST_GROUPS * KEY_VALUE_HEADS, MAX_PROMPT_ROWS + SPAN_TOKENS, HEAD_SIZE)
    all_keys = key_layout(cache_keys, span_rotated_keys)
    all_values = key_layout(prompt_cache_values, span_token_values)
    key_pos = jnp.arange(MAX_PROMPT_ROWS + SPAN_TOKENS, dtype=jnp.int32)
    query_pos = jnp.arange(SPAN_TOKENS, dtype=jnp.int32)

    def single_head(inputs):
        query_rows, head_index = inputs
        key_value_index = head_index // heads_per_group
        key_rows = lax.dynamic_index_in_dim(all_keys, key_value_index, 0, keepdims=False)
        value_rows = lax.dynamic_index_in_dim(all_values, key_value_index, 0, keepdims=False)
        group_length = lax.dynamic_index_in_dim(lengths, key_value_index // KEY_VALUE_HEADS, 0, keepdims=False)
        allowed = jnp.where(key_pos[None, :] < MAX_PROMPT_ROWS, key_pos[None, :] < group_length, key_pos[None, :] - MAX_PROMPT_ROWS <= query_pos[:, None])
        scores = jnp.dot(query_rows, key_rows.T, preferred_element_type=jnp.float32) * score_scale
        scores = jnp.where(allowed, scores, NEG_FILL)
        row_max = lax.optimization_barrier(jnp.max(scores, axis=-1, keepdims=True))
        weights = jnp.where(allowed, jnp.exp(scores - row_max), 0.0)
        row_total = lax.optimization_barrier(jnp.sum(weights, axis=-1, keepdims=True))
        numerator = jnp.dot(weights.astype(jnp.bfloat16), value_rows, preferred_element_type=jnp.float32)
        return (numerator / row_total).astype(jnp.bfloat16)
    per_head_outputs = lax.map(single_head, (query_head_rows, jnp.arange(REQUEST_GROUPS * KEY_VALUE_HEADS * heads_per_group, dtype=jnp.int32)))
    per_head_outputs = per_head_outputs.reshape(REQUEST_GROUPS, KEY_VALUE_HEADS, heads_per_group, SPAN_TOKENS, HEAD_SIZE).transpose(0, 3, 1, 2, 4)
    return per_head_outputs.reshape(REQUEST_GROUPS * SPAN_TOKENS, QUERY_HEADS * HEAD_SIZE)
```

```python
import functools
import math

import jax
import jax.numpy as jnp
from jax import lax
from jax.experimental import pallas as pl
from jax.experimental.pallas import tpu as pltpu
from jax.sharding import PartitionSpec as P

HEAD_SIZE = 128
GROUP_DEVS = 8
NEG_FILL = -1e30
SCALE = 1.0 / math.sqrt(HEAD_SIZE)


def exchange(value, axis, mask):
    pairs = [(source, source ^ mask) for source in range(lax.axis_size(axis))]
    return lax.ppermute(value, axis, pairs)


def gather_group(own):
    half = [member.shape[0] // 2 for member in own]
    from_x = exchange(own, "req", 2)
    from_z = exchange(own, "req", 4)
    diag_lo = exchange(tuple(m[:n] for m, n in zip(from_z, half)), "req", 2)
    diag_hi = exchange(tuple(m[n:] for m, n in zip(from_x, half)), "req", 4)
    diag = tuple(jnp.concatenate([lo, hi], 0) for lo, hi in zip(diag_lo, diag_hi))
    chip = (own, from_x, from_z, diag)
    other = exchange(chip, "req", 1)
    return [own, other[0], from_x, other[1], from_z, other[2], diag, other[3]]


def attn_kernel(info_ref, q_ref, kc_ref, vc_ref, ks_ref, vs_ref, o_ref, m_sc, l_sc, acc_sc):
    step = pl.program_id(0)
    last = pl.num_programs(0) - 1
    n_slots = last
    heads = q_ref.shape[1] // HEAD_SIZE
    tokens = q_ref.shape[0]
    block = kc_ref.shape[0]
    span_block = ks_ref.shape[0]
    length = info_ref[0]
    first_token = info_ref[1]

    @pl.when(step == 0)
    def _init():
        m_sc[...] = jnp.full(m_sc.shape, NEG_FILL, jnp.float32)
        l_sc[...] = jnp.zeros(l_sc.shape, jnp.float32)
        acc_sc[...] = jnp.zeros(acc_sc.shape, jnp.float32)

    def process(k_ref, v_ref, allowed_fn):
        keys = k_ref[...]
        values = v_ref[...]
        allowed = None if allowed_fn is None else allowed_fn()

        def one_head(h, carry):
            col = pl.multiple_of(h * HEAD_SIZE, HEAD_SIZE)
            qh = q_ref[:, pl.ds(col, HEAD_SIZE)]
            s = lax.dot_general(
                qh, keys, (((1,), (1,)), ((), ())), preferred_element_type=jnp.float32
            )
            if allowed is not None:
                s = jnp.where(allowed, s, NEG_FILL)
            m_prev = m_sc[h]
            m_new = jnp.maximum(m_prev, jnp.max(s, axis=1, keepdims=True))
            alpha = jnp.exp((m_prev - m_new) * SCALE)
            p = jnp.exp((s - m_new) * SCALE)
            l_sc[h] = alpha * l_sc[h] + jnp.sum(p, axis=1, keepdims=True)
            pv = jnp.dot(p.astype(jnp.bfloat16), values, preferred_element_type=jnp.float32)
            acc_sc[h] = alpha * acc_sc[h] + pv
            m_sc[h] = m_new
            return carry

        lax.fori_loop(0, heads, one_head, 0)

    @pl.when(step < n_slots)
    def _cache():
        start = info_ref[2 + jnp.minimum(step, n_slots - 1)]
        full = start + block <= length
        partial = jnp.logical_and(start < length, jnp.logical_not(full))

        @pl.when(full)
        def _():
            process(kc_ref, vc_ref, None)

        @pl.when(partial)
        def _():
            def allowed_fn():
                rows = start + lax.broadcasted_iota(jnp.int32, (tokens, block), 1)
                return rows < length

            process(kc_ref, vc_ref, allowed_fn)

    @pl.when(step == n_slots)
    def _span():
        def allowed_fn():
            key_pos = lax.broadcasted_iota(jnp.int32, (tokens, span_block), 1)
            query_pos = first_token + lax.broadcasted_iota(jnp.int32, (tokens, span_block), 0)
            return key_pos <= query_pos

        process(ks_ref, vs_ref, allowed_fn)

    @pl.when(step == last)
    def _finish():
        for h in range(heads):
            o_ref[:, h * HEAD_SIZE:(h + 1) * HEAD_SIZE] = (acc_sc[h] / l_sc[h]).astype(o_ref.dtype)


def attention(info, queries, cache_k, cache_v, span_k, span_v, block):
    tokens, width = queries.shape
    heads = width // HEAD_SIZE
    n_slots = cache_k.shape[0] // block
    span_rows = span_k.shape[0]
    cache_spec = pl.BlockSpec((block, HEAD_SIZE), lambda k, info: (jnp.minimum(k, n_slots - 1), 0))
    span_spec = pl.BlockSpec((span_rows, HEAD_SIZE), lambda k, info: (0, 0))
    whole = pl.BlockSpec((tokens, width), lambda k, info: (0, 0))
    return pl.pallas_call(
        attn_kernel,
        out_shape=jax.ShapeDtypeStruct((tokens, width), jnp.bfloat16),
        grid_spec=pltpu.PrefetchScalarGridSpec(
            num_scalar_prefetch=1,
            grid=(n_slots + 1,),
            in_specs=[whole, cache_spec, cache_spec, span_spec, span_spec],
            out_specs=whole,
            scratch_shapes=[
                pltpu.VMEM((heads, tokens, 1), jnp.float32),
                pltpu.VMEM((heads, tokens, 1), jnp.float32),
                pltpu.VMEM((heads, tokens, HEAD_SIZE), jnp.float32),
            ],
        ),
        compiler_params=pltpu.CompilerParams(
            dimension_semantics=("arbitrary",), vmem_limit_bytes=48 * 1024 * 1024
        ),
    )(info, queries, cache_k, cache_v, span_k, span_v)


def body(queries, span_rotated_keys, span_token_values, cache_keys, prompt_cache_values, lengths):
    tok_rows = queries.shape[0]
    cache_rows = cache_keys.shape[0]
    group_devs = lax.axis_size("req") // lengths.shape[0]
    assert group_devs == GROUP_DEVS
    device = lax.axis_index("req")
    position = device % GROUP_DEVS
    group_length = lax.dynamic_index_in_dim(lengths, device // GROUP_DEVS, 0, keepdims=False)

    slots = gather_group((cache_keys, prompt_cache_values, span_rotated_keys, span_token_values))
    cache_k = jnp.concatenate([slot[0] for slot in slots], 0)
    cache_v = jnp.concatenate([slot[1] for slot in slots], 0)
    order = jnp.arange(GROUP_DEVS, dtype=jnp.int32) ^ position
    span_k = jnp.stack([slot[2] for slot in slots])[order].reshape(-1, HEAD_SIZE)
    span_v = jnp.stack([slot[3] for slot in slots])[order].reshape(-1, HEAD_SIZE)
    starts = (jnp.arange(GROUP_DEVS, dtype=jnp.int32) ^ position) * cache_rows
    info = jnp.concatenate(
        [jnp.stack([group_length, position * tok_rows]).astype(jnp.int32), starts.astype(jnp.int32)]
    )
    attended = attention(info, queries, cache_k, cache_v, span_k, span_v, cache_rows)
    return lax.all_to_all(attended, "tp", split_axis=0, concat_axis=1, tiled=True)


def solution(mesh):
    in_specs = (P("req", "tp"), P("req", "tp"), P("req", "tp"), P("req", "tp"), P("req", "tp"), P())
    out_specs = P(("req", "tp"), None)
    return jax.shard_map(body, mesh=mesh, in_specs=in_specs, out_specs=out_specs, check_vma=False)
```

```python
import math

import jax
import jax.numpy as jnp
from jax import lax
from jax.experimental import pallas as pl
from jax.experimental.pallas import tpu as pltpu
from jax.sharding import PartitionSpec as P

HEAD_SIZE = 128
GROUP_DEVS = 8
NEG_FILL = -1e30
SCALE = 1.0 / math.sqrt(HEAD_SIZE)


def exchange(value, axis, mask):
    pairs = [(source, source ^ mask) for source in range(lax.axis_size(axis))]
    return lax.ppermute(value, axis, pairs)


def gather_group(pack):
    half = pack.shape[0] // 2
    from_x = exchange(pack, "req", 2)
    from_z = exchange(pack, "req", 4)
    diag_lo = exchange(from_z[:half], "req", 2)
    diag_hi = exchange(from_x[half:], "req", 4)
    diag = jnp.concatenate([diag_lo, diag_hi], 0)
    local = jnp.stack([pack, from_x, from_z, diag])
    other = exchange(local, "req", 1)
    return local, other


def attn_kernel(info_ref, q_ref, lk_ref, lv_ref, ls_ref, ok_ref, ov_ref, os_ref, o_ref,
                m_sc, l_sc, acc_sc):
    step = pl.program_id(0)
    last = pl.num_programs(0) - 1
    heads = q_ref.shape[1] // HEAD_SIZE
    tokens = q_ref.shape[0]
    block = lk_ref.shape[0]
    span = ls_ref.shape[0] // 2
    length = info_ref[0]
    first_token = info_ref[1]
    start = info_ref[2 + step]
    span_start = info_ref[2 + GROUP_DEVS + step]

    @pl.when(step == 0)
    def _init():
        m_sc[...] = jnp.full(m_sc.shape, NEG_FILL, jnp.float32)
        l_sc[...] = jnp.zeros(l_sc.shape, jnp.float32)
        acc_sc[...] = jnp.zeros(acc_sc.shape, jnp.float32)

    def process(keys, values, allowed):
        def one_head(h, carry):
            col = pl.multiple_of(h * HEAD_SIZE, HEAD_SIZE)
            qh = q_ref[:, pl.ds(col, HEAD_SIZE)]
            s = lax.dot_general(
                qh, keys, (((1,), (1,)), ((), ())), preferred_element_type=jnp.float32
            )
            if allowed is not None:
                s = jnp.where(allowed, s, NEG_FILL)
            m_prev = m_sc[h]
            m_new = jnp.maximum(m_prev, jnp.max(s, axis=1, keepdims=True))
            alpha = jnp.exp((m_prev - m_new) * SCALE)
            p = jnp.exp((s - m_new) * SCALE)
            l_sc[h] = alpha * l_sc[h] + jnp.sum(p, axis=1, keepdims=True)
            pv = jnp.dot(p.astype(jnp.bfloat16), values, preferred_element_type=jnp.float32)
            acc_sc[h] = alpha * acc_sc[h] + pv
            m_sc[h] = m_new
            return carry

        lax.fori_loop(0, heads, one_head, 0)

    def slot(k_ref, v_ref, s_ref):
        full = start + block <= length
        partial = jnp.logical_and(start < length, jnp.logical_not(full))

        @pl.when(full)
        def _():
            process(k_ref[...], v_ref[...], None)

        @pl.when(partial)
        def _():
            rows = start + lax.broadcasted_iota(jnp.int32, (tokens, block), 1)
            process(k_ref[...], v_ref[...], rows < length)

        @pl.when(span_start < first_token)
        def _():
            process(s_ref[:span], s_ref[span:], None)

        @pl.when(span_start == first_token)
        def _():
            key_pos = lax.broadcasted_iota(jnp.int32, (tokens, span), 1)
            query_pos = lax.broadcasted_iota(jnp.int32, (tokens, span), 0)
            process(s_ref[:span], s_ref[span:], key_pos <= query_pos)

    @pl.when(step % 2 == 0)
    def _local():
        slot(lk_ref, lv_ref, ls_ref)

    @pl.when(step % 2 == 1)
    def _other():
        slot(ok_ref, ov_ref, os_ref)

    @pl.when(step == last)
    def _finish():
        for h in range(heads):
            o_ref[:, h * HEAD_SIZE:(h + 1) * HEAD_SIZE] = (acc_sc[h] / l_sc[h]).astype(o_ref.dtype)


def attention(info, queries, local, other, block, span):
    tokens, width = queries.shape
    heads = width // HEAD_SIZE
    steps = 2 * local.shape[0]
    span_index = 2 * block // (2 * span)

    def views(pick):
        return [
            pl.BlockSpec((None, block, HEAD_SIZE), lambda k, info: (pick(k), 0, 0)),
            pl.BlockSpec((None, block, HEAD_SIZE), lambda k, info: (pick(k), 1, 0)),
            pl.BlockSpec((None, 2 * span, HEAD_SIZE), lambda k, info: (pick(k), span_index, 0)),
        ]

    whole = pl.BlockSpec((tokens, width), lambda k, info: (0, 0))
    in_specs = (
        [whole]
        + views(lambda k: k // 2)
        + views(lambda k: jnp.maximum(k - 1, 0) // 2)
    )
    return pl.pallas_call(
        attn_kernel,
        out_shape=jax.ShapeDtypeStruct((tokens, width), jnp.bfloat16),
        grid_spec=pltpu.PrefetchScalarGridSpec(
            num_scalar_prefetch=1,
            grid=(steps,),
            in_specs=in_specs,
            out_specs=whole,
            scratch_shapes=[
                pltpu.VMEM((heads, tokens, 1), jnp.float32),
                pltpu.VMEM((heads, tokens, 1), jnp.float32),
                pltpu.VMEM((heads, tokens, HEAD_SIZE), jnp.float32),
            ],
        ),
        compiler_params=pltpu.CompilerParams(
            dimension_semantics=("arbitrary",), vmem_limit_bytes=48 * 1024 * 1024
        ),
    )(info, queries, local, local, local, other, other, other)


def body(queries, span_rotated_keys, span_token_values, cache_keys, prompt_cache_values, lengths):
    tok_rows = queries.shape[0]
    cache_rows = cache_keys.shape[0]
    group_devs = lax.axis_size("req") // lengths.shape[0]
    assert group_devs == GROUP_DEVS
    assert span_rotated_keys.shape[0] * 2 * 4 == cache_rows
    device = lax.axis_index("req")
    position = device % GROUP_DEVS
    group_length = lax.dynamic_index_in_dim(lengths, device // GROUP_DEVS, 0, keepdims=False)

    pack = jnp.concatenate(
        [cache_keys, prompt_cache_values, span_rotated_keys, span_token_values], 0
    )
    local, other = gather_group(pack)
    slot_pos = jnp.arange(GROUP_DEVS, dtype=jnp.int32) ^ position
    info = jnp.concatenate(
        [
            jnp.stack([group_length, position * tok_rows]).astype(jnp.int32),
            (slot_pos * cache_rows).astype(jnp.int32),
            (slot_pos * tok_rows).astype(jnp.int32),
        ]
    )
    attended = attention(info, queries, local, other, cache_rows, span_rotated_keys.shape[0])
    return lax.all_to_all(attended, "tp", split_axis=0, concat_axis=1, tiled=True)


def solution(mesh):
    in_specs = (P("req", "tp"), P("req", "tp"), P("req", "tp"), P("req", "tp"), P("req", "tp"), P())
    out_specs = P(("req", "tp"), None)
    return jax.shard_map(body, mesh=mesh, in_specs=in_specs, out_specs=out_specs, check_vma=False)
```

```python
import math

import jax
import jax.numpy as jnp
from jax import lax
from jax.experimental import pallas as pl
from jax.experimental.pallas import tpu as pltpu
from jax.sharding import PartitionSpec as P

HEAD_SIZE = 128
GROUP_DEVS = 8
NEG_FILL = -1e30
SCALE = 1.0 / math.sqrt(HEAD_SIZE)


def exchange(value, axis, mask):
    pairs = [(source, source ^ mask) for source in range(lax.axis_size(axis))]
    return lax.ppermute(value, axis, pairs)


def gather_group(pack):
    half = pack.shape[0] // 2
    from_x = exchange(pack, "req", 2)
    from_z = exchange(pack, "req", 4)
    diag_lo = exchange(from_z[:half], "req", 2)
    diag_hi = exchange(from_x[half:], "req", 4)
    diag = jnp.concatenate([diag_lo, diag_hi], 0)
    local = jnp.stack([pack, from_x, from_z, diag])
    other = exchange(local, "req", 1)
    return local, other


def attn_kernel(info_ref, q_ref, lk_ref, lv_ref, ok_ref, ov_ref, sk_ref, sv_ref, o_ref,
                m_sc, l_sc, acc_sc):
    step = pl.program_id(0)
    last = pl.num_programs(0) - 1
    rows = q_ref.shape[0]
    tokens = o_ref.shape[0]
    heads = rows // tokens
    block = lk_ref.shape[0]
    span = sk_ref.shape[0]
    length = info_ref[0]
    first_token = info_ref[1]
    start = info_ref[2 + jnp.minimum(step, last - 1)]

    @pl.when(step == 0)
    def _init():
        m_sc[...] = jnp.full(m_sc.shape, NEG_FILL, jnp.float32)
        l_sc[...] = jnp.zeros(l_sc.shape, jnp.float32)
        acc_sc[...] = jnp.zeros(acc_sc.shape, jnp.float32)

    def process(keys, values, allowed):
        s = lax.dot_general(
            q_ref[...], keys, (((1,), (1,)), ((), ())), preferred_element_type=jnp.float32
        )
        if allowed is not None:
            s = jnp.where(allowed, s, NEG_FILL)
        m_prev = m_sc[...]
        m_new = jnp.maximum(m_prev, jnp.max(s, axis=1, keepdims=True))
        alpha = jnp.exp((m_prev - m_new) * SCALE)
        p = jnp.exp((s - m_new) * SCALE)
        l_sc[...] = alpha * l_sc[...] + jnp.sum(p, axis=1, keepdims=True)
        pv = jnp.dot(p.astype(jnp.bfloat16), values, preferred_element_type=jnp.float32)
        acc_sc[...] = alpha * acc_sc[...] + pv
        m_sc[...] = m_new

    def slot(k_ref, v_ref):
        full = start + block <= length
        partial = jnp.logical_and(start < length, jnp.logical_not(full))

        @pl.when(full)
        def _():
            process(k_ref[...], v_ref[...], None)

        @pl.when(partial)
        def _():
            key_rows = start + lax.broadcasted_iota(jnp.int32, (rows, block), 1)
            process(k_ref[...], v_ref[...], key_rows < length)

    @pl.when(jnp.logical_and(step < last, step % 2 == 0))
    def _local():
        slot(lk_ref, lv_ref)

    @pl.when(jnp.logical_and(step < last, step % 2 == 1))
    def _other():
        slot(ok_ref, ov_ref)

    @pl.when(step == last)
    def _span():
        key_pos = lax.broadcasted_iota(jnp.int32, (rows, span), 1)
        query_pos = first_token + lax.rem(lax.broadcasted_iota(jnp.int32, (rows, span), 0), tokens)
        process(sk_ref[...], sv_ref[...], key_pos <= query_pos)

    @pl.when(step == last)
    def _finish():
        for h in range(heads):
            rows_h = slice(h * tokens, (h + 1) * tokens)
            o_ref[:, h * HEAD_SIZE:(h + 1) * HEAD_SIZE] = (
                acc_sc[rows_h, :] / l_sc[rows_h, :]
            ).astype(o_ref.dtype)


def attention(info, q_rows, local, other, span_k, span_v, block, tokens):
    rows = q_rows.shape[0]
    heads = rows // tokens
    width = heads * HEAD_SIZE
    slots = 2 * local.shape[0]
    span = span_k.shape[0]

    def views(pick):
        return [
            pl.BlockSpec((None, block, HEAD_SIZE), lambda k, info: (pick(jnp.minimum(k, slots - 1)), 0, 0)),
            pl.BlockSpec((None, block, HEAD_SIZE), lambda k, info: (pick(jnp.minimum(k, slots - 1)), 1, 0)),
        ]

    fixed = lambda k, info: (0, 0)
    in_specs = (
        [pl.BlockSpec((rows, HEAD_SIZE), fixed)]
        + views(lambda k: k // 2)
        + views(lambda k: jnp.maximum(k - 1, 0) // 2)
        + [pl.BlockSpec((span, HEAD_SIZE), fixed), pl.BlockSpec((span, HEAD_SIZE), fixed)]
    )
    return pl.pallas_call(
        attn_kernel,
        out_shape=jax.ShapeDtypeStruct((tokens, width), jnp.bfloat16),
        grid_spec=pltpu.PrefetchScalarGridSpec(
            num_scalar_prefetch=1,
            grid=(slots + 1,),
            in_specs=in_specs,
            out_specs=pl.BlockSpec((tokens, width), fixed),
            scratch_shapes=[
                pltpu.VMEM((rows, 1), jnp.float32),
                pltpu.VMEM((rows, 1), jnp.float32),
                pltpu.VMEM((rows, HEAD_SIZE), jnp.float32),
            ],
        ),
        compiler_params=pltpu.CompilerParams(
            dimension_semantics=("arbitrary",), vmem_limit_bytes=56 * 1024 * 1024
        ),
    )(info, q_rows, local, local, other, other, span_k, span_v)


def heads_as_rows(queries):
    tokens, width = queries.shape
    heads = width // HEAD_SIZE
    return queries.reshape(tokens, heads, HEAD_SIZE).transpose(1, 0, 2).reshape(heads * tokens, HEAD_SIZE)


def body(queries, span_rotated_keys, span_token_values, cache_keys, prompt_cache_values, lengths):
    tok_rows = queries.shape[0]
    cache_rows = cache_keys.shape[0]
    group_devs = lax.axis_size("req") // lengths.shape[0]
    assert group_devs == GROUP_DEVS
    device = lax.axis_index("req")
    position = device % GROUP_DEVS
    group_length = lax.dynamic_index_in_dim(lengths, device // GROUP_DEVS, 0, keepdims=False)

    pack = jnp.concatenate(
        [cache_keys, prompt_cache_values, span_rotated_keys, span_token_values], 0
    )
    local, other = gather_group(pack)
    slot_pos = jnp.arange(GROUP_DEVS, dtype=jnp.int32) ^ position
    info = jnp.concatenate(
        [
            jnp.stack([group_length, position * tok_rows]).astype(jnp.int32),
            (slot_pos * cache_rows).astype(jnp.int32),
        ]
    )
    span_rows = span_rotated_keys.shape[0]
    span_cut = 2 * cache_rows
    by_slot = jnp.stack([local[:, span_cut:], other[:, span_cut:]], 1)
    by_position = by_slot.reshape(GROUP_DEVS, 2 * span_rows, HEAD_SIZE)[slot_pos]
    span_k = by_position[:, :span_rows].reshape(-1, HEAD_SIZE)
    span_v = by_position[:, span_rows:].reshape(-1, HEAD_SIZE)
    attended = attention(
        info, heads_as_rows(queries), local, other, span_k, span_v, cache_rows, tok_rows
    )
    return lax.all_to_all(attended, "tp", split_axis=0, concat_axis=1, tiled=True)


def solution(mesh):
    in_specs = (P("req", "tp"), P("req", "tp"), P("req", "tp"), P("req", "tp"), P("req", "tp"), P())
    out_specs = P(("req", "tp"), None)
    return jax.shard_map(body, mesh=mesh, in_specs=in_specs, out_specs=out_specs, check_vma=False)
```

```python
import math

import jax
import jax.numpy as jnp
from jax import lax
from jax.experimental import pallas as pl
from jax.experimental.pallas import tpu as pltpu
from jax.sharding import Mesh, PartitionSpec as P

HEAD_SIZE = 128
GROUP_DEVS = 8
GROUP_COUNT = 8
NEG_FILL = -1e30
SCALE = 1.0 / math.sqrt(HEAD_SIZE)


def attn_kernel(info_ref, q_ref, k_ref, v_ref, sk_ref, sv_ref, o_ref, m_sc, l_sc, acc_sc):
    step = pl.program_id(0)
    last = pl.num_programs(0) - 1
    rows = q_ref.shape[0]
    tokens = o_ref.shape[0]
    heads = rows // tokens
    block = k_ref.shape[0]
    span = sk_ref.shape[0]
    length = info_ref[0]
    first_token = info_ref[1]
    start = step * block

    @pl.when(step == 0)
    def _init():
        m_sc[...] = jnp.full(m_sc.shape, NEG_FILL, jnp.float32)
        l_sc[...] = jnp.zeros(l_sc.shape, jnp.float32)
        acc_sc[...] = jnp.zeros(acc_sc.shape, jnp.float32)

    def process(keys, values, allowed):
        s = lax.dot_general(
            q_ref[...], keys, (((1,), (1,)), ((), ())), preferred_element_type=jnp.float32
        )
        if allowed is not None:
            s = jnp.where(allowed, s, NEG_FILL)
        m_prev = m_sc[...]
        m_new = jnp.maximum(m_prev, jnp.max(s, axis=1, keepdims=True))
        alpha = jnp.exp((m_prev - m_new) * SCALE)
        p = jnp.exp((s - m_new) * SCALE)
        l_sc[...] = alpha * l_sc[...] + jnp.sum(p, axis=1, keepdims=True)
        pv = jnp.dot(p.astype(jnp.bfloat16), values, preferred_element_type=jnp.float32)
        acc_sc[...] = alpha * acc_sc[...] + pv
        m_sc[...] = m_new

    def slot(k_ref, v_ref):
        full = start + block <= length
        partial = jnp.logical_and(start < length, jnp.logical_not(full))

        @pl.when(full)
        def _():
            process(k_ref[...], v_ref[...], None)

        @pl.when(partial)
        def _():
            key_rows = start + lax.broadcasted_iota(jnp.int32, (rows, block), 1)
            process(k_ref[...], v_ref[...], key_rows < length)

    @pl.when(step < last)
    def _cache():
        slot(k_ref, v_ref)

    @pl.when(step == last)
    def _span():
        key_pos = lax.broadcasted_iota(jnp.int32, (rows, span), 1)
        query_pos = first_token + lax.rem(lax.broadcasted_iota(jnp.int32, (rows, span), 0), tokens)
        process(sk_ref[...], sv_ref[...], key_pos <= query_pos)

    @pl.when(step == last)
    def _finish():
        for h in range(heads):
            rows_h = slice(h * tokens, (h + 1) * tokens)
            o_ref[:, h * HEAD_SIZE:(h + 1) * HEAD_SIZE] = (
                acc_sc[rows_h, :] / l_sc[rows_h, :]
            ).astype(o_ref.dtype)


def attention(info, q_rows, packs, span_k, span_v, block, tokens):
    rows = q_rows.shape[0]
    heads = rows // tokens
    width = heads * HEAD_SIZE
    slots = packs.shape[0]
    span = span_k.shape[0]
    fixed = lambda k, info: (0, 0)
    in_specs = [
        pl.BlockSpec((rows, HEAD_SIZE), fixed),
        pl.BlockSpec((None, block, HEAD_SIZE), lambda k, info: (jnp.minimum(k, slots - 1), 0, 0)),
        pl.BlockSpec((None, block, HEAD_SIZE), lambda k, info: (jnp.minimum(k, slots - 1), 1, 0)),
        pl.BlockSpec((span, HEAD_SIZE), fixed),
        pl.BlockSpec((span, HEAD_SIZE), fixed),
    ]
    return pl.pallas_call(
        attn_kernel,
        out_shape=jax.ShapeDtypeStruct((tokens, width), jnp.bfloat16),
        grid_spec=pltpu.PrefetchScalarGridSpec(
            num_scalar_prefetch=1,
            grid=(slots + 1,),
            in_specs=in_specs,
            out_specs=pl.BlockSpec((tokens, width), fixed),
            scratch_shapes=[
                pltpu.VMEM((rows, 1), jnp.float32),
                pltpu.VMEM((rows, 1), jnp.float32),
                pltpu.VMEM((rows, HEAD_SIZE), jnp.float32),
            ],
        ),
        compiler_params=pltpu.CompilerParams(
            dimension_semantics=("arbitrary",), vmem_limit_bytes=56 * 1024 * 1024
        ),
    )(info, q_rows, packs, packs, span_k, span_v)


def heads_as_rows(queries):
    tokens, width = queries.shape
    heads = width // HEAD_SIZE
    return queries.reshape(tokens, heads, HEAD_SIZE).transpose(1, 0, 2).reshape(heads * tokens, HEAD_SIZE)


def body(queries, span_rotated_keys, span_token_values, cache_keys, prompt_cache_values, lengths):
    tok_rows = queries.shape[0]
    cache_rows = cache_keys.shape[0]
    span_rows = span_rotated_keys.shape[0]
    position = lax.axis_index("pos")
    group_length = lax.dynamic_index_in_dim(lengths, lax.axis_index("grp"), 0, keepdims=False)

    pack = jnp.concatenate(
        [cache_keys, prompt_cache_values, span_rotated_keys, span_token_values], 0
    )
    packs = lax.all_gather(pack, "pos")
    info = jnp.stack([group_length, position * tok_rows]).astype(jnp.int32)
    span_cut = 2 * cache_rows
    span_k = packs[:, span_cut:span_cut + span_rows].reshape(-1, HEAD_SIZE)
    span_v = packs[:, span_cut + span_rows:].reshape(-1, HEAD_SIZE)
    attended = attention(info, heads_as_rows(queries), packs, span_k, span_v, cache_rows, tok_rows)
    return lax.all_to_all(attended, "tp", split_axis=0, concat_axis=1, tiled=True)


def solution(mesh):
    groups = GROUP_COUNT
    req = mesh.shape["req"]
    devices = mesh.devices.reshape(groups, req // groups, mesh.shape["tp"])
    group_mesh = Mesh(devices, ("grp", "pos", "tp"))
    rows = P(("grp", "pos"), "tp")
    in_specs = (rows, rows, rows, rows, rows, P())
    out_specs = P(("grp", "pos", "tp"), None)
    return jax.shard_map(
        body, mesh=group_mesh, in_specs=in_specs, out_specs=out_specs, check_vma=False
    )
```

```python
import math

import jax
import jax.numpy as jnp
from jax import lax
from jax.experimental import pallas as pl
from jax.experimental.pallas import tpu as pltpu
from jax.sharding import PartitionSpec as P

HEAD_SIZE = 128
GROUP_DEVS = 8
NEG_FILL = -1e30
SCALE = 1.0 / math.sqrt(HEAD_SIZE)


def exchange(value, axis, mask):
    pairs = [(source, source ^ mask) for source in range(lax.axis_size(axis))]
    return lax.ppermute(value, axis, pairs)


def gather_group(pack):
    half = pack.shape[0] // 2
    from_x = exchange(pack, "req", 2)
    from_z = exchange(pack, "req", 4)
    diag_lo = exchange(from_z[:half], "req", 2)
    diag_hi = exchange(from_x[half:], "req", 4)
    diag = jnp.concatenate([diag_lo, diag_hi], 0)
    local = jnp.stack([pack, from_x, from_z, diag])
    other = exchange(local, "req", 1)
    return local, other


def span_copies(info_ref, local_any, other_any, sk_sc, sv_sc, sems, block, span):
    copies = []
    for j in range(local_any.shape[0]):
        for parity, source in ((0, local_any), (1, other_any)):
            slot = 2 * j + parity
            offset = pl.multiple_of(info_ref[2 + GROUP_DEVS + slot], span)
            for part, target in ((0, sk_sc), (1, sv_sc)):
                copies.append(
                    pltpu.make_async_copy(
                        source.at[j, pl.ds(2 * block + part * span, span), :],
                        target.at[pl.ds(offset, span), :],
                        sems.at[2 * slot + part],
                    )
                )
    return copies


def attn_kernel(info_ref, q_ref, lk_ref, lv_ref, ok_ref, ov_ref, la_ref, oa_ref, o_ref,
                m_sc, l_sc, acc_sc, sk_sc, sv_sc, sems):
    step = pl.program_id(0)
    last = pl.num_programs(0) - 1
    rows = q_ref.shape[0]
    tokens = o_ref.shape[0]
    heads = rows // tokens
    block = lk_ref.shape[0]
    span = sk_sc.shape[0] // GROUP_DEVS
    length = info_ref[0]
    first_token = info_ref[1]
    start = info_ref[2 + jnp.minimum(step, last - 1)]

    @pl.when(step == 0)
    def _init():
        for copy in span_copies(info_ref, la_ref, oa_ref, sk_sc, sv_sc, sems, block, span):
            copy.start()
        m_sc[...] = jnp.full(m_sc.shape, NEG_FILL, jnp.float32)
        l_sc[...] = jnp.zeros(l_sc.shape, jnp.float32)
        acc_sc[...] = jnp.zeros(acc_sc.shape, jnp.float32)

    def process(keys, values, allowed):
        s = lax.dot_general(
            q_ref[...], keys, (((1,), (1,)), ((), ())), preferred_element_type=jnp.float32
        )
        if allowed is not None:
            s = jnp.where(allowed, s, NEG_FILL)
        m_prev = m_sc[...]
        m_new = jnp.maximum(m_prev, jnp.max(s, axis=1, keepdims=True))
        alpha = jnp.exp((m_prev - m_new) * SCALE)
        p = jnp.exp((s - m_new) * SCALE)
        l_sc[...] = alpha * l_sc[...] + jnp.sum(p, axis=1, keepdims=True)
        pv = jnp.dot(p.astype(jnp.bfloat16), values, preferred_element_type=jnp.float32)
        acc_sc[...] = alpha * acc_sc[...] + pv
        m_sc[...] = m_new

    def slot(k_ref, v_ref):
        full = start + block <= length
        partial = jnp.logical_and(start < length, jnp.logical_not(full))

        @pl.when(full)
        def _():
            process(k_ref[...], v_ref[...], None)

        @pl.when(partial)
        def _():
            key_rows = start + lax.broadcasted_iota(jnp.int32, (rows, block), 1)
            process(k_ref[...], v_ref[...], key_rows < length)

    @pl.when(jnp.logical_and(step < last, step % 2 == 0))
    def _local():
        slot(lk_ref, lv_ref)

    @pl.when(jnp.logical_and(step < last, step % 2 == 1))
    def _other():
        slot(ok_ref, ov_ref)

    @pl.when(step == last)
    def _span():
        for copy in span_copies(info_ref, la_ref, oa_ref, sk_sc, sv_sc, sems, block, span):
            copy.wait()
        span_rows = sk_sc.shape[0]
        key_pos = lax.broadcasted_iota(jnp.int32, (rows, span_rows), 1)
        query_pos = first_token + lax.rem(lax.broadcasted_iota(jnp.int32, (rows, span_rows), 0), tokens)
        process(sk_sc[...], sv_sc[...], key_pos <= query_pos)

    @pl.when(step == last)
    def _finish():
        for h in range(heads):
            rows_h = slice(h * tokens, (h + 1) * tokens)
            o_ref[:, h * HEAD_SIZE:(h + 1) * HEAD_SIZE] = (
                acc_sc[rows_h, :] / l_sc[rows_h, :]
            ).astype(o_ref.dtype)


def attention(info, q_rows, local, other, block, span, tokens):
    rows = q_rows.shape[0]
    heads = rows // tokens
    width = heads * HEAD_SIZE
    slots = 2 * local.shape[0]

    def views(pick):
        return [
            pl.BlockSpec((None, block, HEAD_SIZE), lambda k, info: (pick(jnp.minimum(k, slots - 1)), 0, 0)),
            pl.BlockSpec((None, block, HEAD_SIZE), lambda k, info: (pick(jnp.minimum(k, slots - 1)), 1, 0)),
        ]

    fixed = lambda k, info: (0, 0)
    in_specs = (
        [pl.BlockSpec((rows, HEAD_SIZE), fixed)]
        + views(lambda k: k // 2)
        + views(lambda k: jnp.maximum(k - 1, 0) // 2)
        + [pl.BlockSpec(memory_space=pl.ANY), pl.BlockSpec(memory_space=pl.ANY)]
    )
    return pl.pallas_call(
        attn_kernel,
        out_shape=jax.ShapeDtypeStruct((tokens, width), jnp.bfloat16),
        grid_spec=pltpu.PrefetchScalarGridSpec(
            num_scalar_prefetch=1,
            grid=(slots + 1,),
            in_specs=in_specs,
            out_specs=pl.BlockSpec((tokens, width), fixed),
            scratch_shapes=[
                pltpu.VMEM((rows, 1), jnp.float32),
                pltpu.VMEM((rows, 1), jnp.float32),
                pltpu.VMEM((rows, HEAD_SIZE), jnp.float32),
                pltpu.VMEM((slots * span, HEAD_SIZE), jnp.bfloat16),
                pltpu.VMEM((slots * span, HEAD_SIZE), jnp.bfloat16),
                pltpu.SemaphoreType.DMA((4 * slots,)),
            ],
        ),
        compiler_params=pltpu.CompilerParams(
            dimension_semantics=("arbitrary",), vmem_limit_bytes=56 * 1024 * 1024
        ),
    )(info, q_rows, local, local, other, other, local, other)


def pack_kernel(k_ref, v_ref, sk_ref, sv_ref, o_ref):
    rows = k_ref.shape[0]
    span = sk_ref.shape[0]
    o_ref[0:rows, :] = k_ref[...]
    o_ref[rows:2 * rows, :] = v_ref[...]
    o_ref[2 * rows:2 * rows + span, :] = sk_ref[...]
    o_ref[2 * rows + span:2 * rows + 2 * span, :] = sv_ref[...]


def make_pack(cache_k, cache_v, span_k, span_v):
    rows = 2 * cache_k.shape[0] + 2 * span_k.shape[0]
    return pl.pallas_call(
        pack_kernel,
        out_shape=jax.ShapeDtypeStruct((rows, HEAD_SIZE), cache_k.dtype),
    )(cache_k, cache_v, span_k, span_v)


def heads_as_rows(queries):
    tokens, width = queries.shape
    heads = width // HEAD_SIZE
    return queries.reshape(tokens, heads, HEAD_SIZE).transpose(1, 0, 2).reshape(heads * tokens, HEAD_SIZE)


def body(queries, span_rotated_keys, span_token_values, cache_keys, prompt_cache_values, lengths):
    tok_rows = queries.shape[0]
    cache_rows = cache_keys.shape[0]
    group_devs = lax.axis_size("req") // lengths.shape[0]
    assert group_devs == GROUP_DEVS
    device = lax.axis_index("req")
    position = device % GROUP_DEVS
    group_length = lax.dynamic_index_in_dim(lengths, device // GROUP_DEVS, 0, keepdims=False)

    pack = make_pack(cache_keys, prompt_cache_values, span_rotated_keys, span_token_values)
    local, other = gather_group(pack)
    slot_pos = jnp.arange(GROUP_DEVS, dtype=jnp.int32) ^ position
    span_rows = span_rotated_keys.shape[0]
    info = jnp.concatenate(
        [
            jnp.stack([group_length, position * tok_rows]).astype(jnp.int32),
            (slot_pos * cache_rows).astype(jnp.int32),
            (slot_pos * span_rows).astype(jnp.int32),
        ]
    )
    attended = attention(info, heads_as_rows(queries), local, other, cache_rows, span_rows, tok_rows)
    return lax.all_to_all(attended, "tp", split_axis=0, concat_axis=1, tiled=True)


def solution(mesh):
    in_specs = (P("req", "tp"), P("req", "tp"), P("req", "tp"), P("req", "tp"), P("req", "tp"), P())
    out_specs = P(("req", "tp"), None)
    return jax.shard_map(body, mesh=mesh, in_specs=in_specs, out_specs=out_specs, check_vma=False)
```

```python
import math

import jax
import jax.numpy as jnp
from jax import lax
from jax.experimental import pallas as pl
from jax.experimental.pallas import tpu as pltpu
from jax.sharding import PartitionSpec as P

HEAD_SIZE = 128
GROUP_DEVS = 8
NEG_FILL = -1e30
SCALE = 1.0 / math.sqrt(HEAD_SIZE)
EXP2_SCALE = SCALE * math.log2(math.e)


def exchange(value, axis, mask):
    pairs = [(source, source ^ mask) for source in range(lax.axis_size(axis))]
    return lax.ppermute(value, axis, pairs)


def gather_group(pack):
    half = pack.shape[0] // 2
    from_x = exchange(pack, "req", 2)
    from_z = exchange(pack, "req", 4)
    diag_lo = exchange(from_z[:half], "req", 2)
    diag_hi = exchange(from_x[half:], "req", 4)
    diag = jnp.concatenate([diag_lo, diag_hi], 0)
    local = jnp.stack([pack, from_x, from_z, diag])
    other = exchange(local, "req", 1)
    return local, other


def span_copies(info_ref, local_any, other_any, sk_sc, sv_sc, sems, block, span):
    copies = []
    for j in range(local_any.shape[0]):
        for parity, source in ((0, local_any), (1, other_any)):
            slot = 2 * j + parity
            offset = pl.multiple_of(info_ref[2 + GROUP_DEVS + slot], span)
            for part, target in ((0, sk_sc), (1, sv_sc)):
                copies.append(
                    pltpu.make_async_copy(
                        source.at[j, pl.ds(2 * block + part * span, span), :],
                        target.at[pl.ds(offset, span), :],
                        sems.at[2 * slot + part],
                    )
                )
    return copies


def attn_kernel(info_ref, q_ref, lk_ref, lv_ref, ok_ref, ov_ref, la_ref, oa_ref, o_ref,
                m_sc, l_sc, acc_sc, sk_sc, sv_sc, sems):
    step = pl.program_id(0)
    last = pl.num_programs(0) - 1
    rows = q_ref.shape[0]
    tokens = o_ref.shape[0]
    heads = rows // tokens
    block = lk_ref.shape[0]
    span = sk_sc.shape[0] // GROUP_DEVS
    length = info_ref[0]
    first_token = info_ref[1]
    start = info_ref[2 + jnp.minimum(step, last - 1)]

    @pl.when(step == 0)
    def _init():
        for copy in span_copies(info_ref, la_ref, oa_ref, sk_sc, sv_sc, sems, block, span):
            copy.start()
        m_sc[...] = jnp.full(m_sc.shape, NEG_FILL, jnp.float32)
        l_sc[...] = jnp.zeros(l_sc.shape, jnp.float32)
        acc_sc[...] = jnp.zeros(acc_sc.shape, jnp.float32)

    def process(keys, values, allowed):
        s = lax.dot_general(
            q_ref[...], keys, (((1,), (1,)), ((), ())), preferred_element_type=jnp.float32
        )
        if allowed is not None:
            s = jnp.where(allowed, s, NEG_FILL)
        m_prev = m_sc[...]
        m_new = jnp.maximum(m_prev, jnp.max(s, axis=1, keepdims=True))
        alpha = jnp.exp2((m_prev - m_new) * EXP2_SCALE)
        p = jnp.exp2((s - m_new) * EXP2_SCALE)
        l_sc[...] = alpha * l_sc[...] + jnp.sum(p, axis=1, keepdims=True)
        pv = jnp.dot(p.astype(jnp.bfloat16), values, preferred_element_type=jnp.float32)
        acc_sc[...] = alpha * acc_sc[...] + pv
        m_sc[...] = m_new

    def slot(k_ref, v_ref):
        full = start + block <= length
        partial = jnp.logical_and(start < length, jnp.logical_not(full))

        @pl.when(full)
        def _():
            process(k_ref[...], v_ref[...], None)

        @pl.when(partial)
        def _():
            key_rows = start + lax.broadcasted_iota(jnp.int32, (rows, block), 1)
            process(k_ref[...], v_ref[...], key_rows < length)

    @pl.when(jnp.logical_and(step < last, step % 2 == 0))
    def _local():
        slot(lk_ref, lv_ref)

    @pl.when(jnp.logical_and(step < last, step % 2 == 1))
    def _other():
        slot(ok_ref, ov_ref)

    @pl.when(step == last)
    def _span():
        for copy in span_copies(info_ref, la_ref, oa_ref, sk_sc, sv_sc, sems, block, span):
            copy.wait()
        span_rows = sk_sc.shape[0]
        key_pos = lax.broadcasted_iota(jnp.int32, (rows, span_rows), 1)
        query_pos = first_token + lax.rem(lax.broadcasted_iota(jnp.int32, (rows, span_rows), 0), tokens)
        process(sk_sc[...], sv_sc[...], key_pos <= query_pos)

    @pl.when(step == last)
    def _finish():
        for h in range(heads):
            rows_h = slice(h * tokens, (h + 1) * tokens)
            o_ref[:, h * HEAD_SIZE:(h + 1) * HEAD_SIZE] = (
                acc_sc[rows_h, :] / l_sc[rows_h, :]
            ).astype(o_ref.dtype)


def attention(info, q_rows, local, other, block, span, tokens):
    rows = q_rows.shape[0]
    heads = rows // tokens
    width = heads * HEAD_SIZE
    slots = 2 * local.shape[0]

    def views(pick):
        return [
            pl.BlockSpec((None, block, HEAD_SIZE), lambda k, info: (pick(jnp.minimum(k, slots - 1)), 0, 0)),
            pl.BlockSpec((None, block, HEAD_SIZE), lambda k, info: (pick(jnp.minimum(k, slots - 1)), 1, 0)),
        ]

    fixed = lambda k, info: (0, 0)
    in_specs = (
        [pl.BlockSpec((rows, HEAD_SIZE), fixed)]
        + views(lambda k: k // 2)
        + views(lambda k: jnp.maximum(k - 1, 0) // 2)
        + [pl.BlockSpec(memory_space=pl.ANY), pl.BlockSpec(memory_space=pl.ANY)]
    )
    return pl.pallas_call(
        attn_kernel,
        out_shape=jax.ShapeDtypeStruct((tokens, width), jnp.bfloat16),
        grid_spec=pltpu.PrefetchScalarGridSpec(
            num_scalar_prefetch=1,
            grid=(slots + 1,),
            in_specs=in_specs,
            out_specs=pl.BlockSpec((tokens, width), fixed),
            scratch_shapes=[
                pltpu.VMEM((rows, 1), jnp.float32),
                pltpu.VMEM((rows, 1), jnp.float32),
                pltpu.VMEM((rows, HEAD_SIZE), jnp.float32),
                pltpu.VMEM((slots * span, HEAD_SIZE), jnp.bfloat16),
                pltpu.VMEM((slots * span, HEAD_SIZE), jnp.bfloat16),
                pltpu.SemaphoreType.DMA((4 * slots,)),
            ],
        ),
        compiler_params=pltpu.CompilerParams(
            dimension_semantics=("arbitrary",), vmem_limit_bytes=56 * 1024 * 1024
        ),
    )(info, q_rows, local, local, other, other, local, other)


def pack_kernel(k_ref, v_ref, sk_ref, sv_ref, o_ref):
    rows = k_ref.shape[0]
    span = sk_ref.shape[0]
    o_ref[0:rows, :] = k_ref[...]
    o_ref[rows:2 * rows, :] = v_ref[...]
    o_ref[2 * rows:2 * rows + span, :] = sk_ref[...]
    o_ref[2 * rows + span:2 * rows + 2 * span, :] = sv_ref[...]


def make_pack(cache_k, cache_v, span_k, span_v):
    rows = 2 * cache_k.shape[0] + 2 * span_k.shape[0]
    return pl.pallas_call(
        pack_kernel,
        out_shape=jax.ShapeDtypeStruct((rows, HEAD_SIZE), cache_k.dtype),
    )(cache_k, cache_v, span_k, span_v)


def heads_as_rows(queries):
    tokens, width = queries.shape
    heads = width // HEAD_SIZE
    return queries.reshape(tokens, heads, HEAD_SIZE).transpose(1, 0, 2).reshape(heads * tokens, HEAD_SIZE)


def body(queries, span_rotated_keys, span_token_values, cache_keys, prompt_cache_values, lengths):
    tok_rows = queries.shape[0]
    cache_rows = cache_keys.shape[0]
    group_devs = lax.axis_size("req") // lengths.shape[0]
    assert group_devs == GROUP_DEVS
    device = lax.axis_index("req")
    position = device % GROUP_DEVS
    group_length = lax.dynamic_index_in_dim(lengths, device // GROUP_DEVS, 0, keepdims=False)

    pack = make_pack(cache_keys, prompt_cache_values, span_rotated_keys, span_token_values)
    local, other = gather_group(pack)
    slot_pos = jnp.arange(GROUP_DEVS, dtype=jnp.int32) ^ position
    span_rows = span_rotated_keys.shape[0]
    info = jnp.concatenate(
        [
            jnp.stack([group_length, position * tok_rows]).astype(jnp.int32),
            (slot_pos * cache_rows).astype(jnp.int32),
            (slot_pos * span_rows).astype(jnp.int32),
        ]
    )
    attended = attention(info, heads_as_rows(queries), local, other, cache_rows, span_rows, tok_rows)
    return lax.all_to_all(attended, "tp", split_axis=0, concat_axis=1, tiled=True)


def solution(mesh):
    in_specs = (P("req", "tp"), P("req", "tp"), P("req", "tp"), P("req", "tp"), P("req", "tp"), P())
    out_specs = P(("req", "tp"), None)
    return jax.shard_map(body, mesh=mesh, in_specs=in_specs, out_specs=out_specs, check_vma=False)
```

```python
import math

import jax
import jax.numpy as jnp
from jax import lax
from jax.experimental import pallas as pl
from jax.experimental.pallas import tpu as pltpu
from jax.sharding import PartitionSpec as P

HEAD_SIZE = 128
GROUP_DEVS = 8
NEG_FILL = -1e30
SCALE = 1.0 / math.sqrt(HEAD_SIZE)
EXP2_SCALE = SCALE * math.log2(math.e)


def exchange(value, axis, mask):
    pairs = [(source, source ^ mask) for source in range(lax.axis_size(axis))]
    return lax.ppermute(value, axis, pairs)


def gather_group(pack):
    half = pack.shape[0] // 2
    from_x = exchange(pack, "req", 2)
    from_z = exchange(pack, "req", 4)
    diag_lo = exchange(from_z[:half], "req", 2)
    diag_hi = exchange(from_x[half:], "req", 4)
    diag = jnp.concatenate([diag_lo, diag_hi], 0)
    local = jnp.stack([pack, from_x, from_z, diag])
    other = exchange(local, "req", 1)
    return local, other


def span_copies(info_ref, local_any, other_any, sk_sc, sv_sc, sems, block, span):
    copies = []
    for j in range(local_any.shape[0]):
        for parity, source in ((0, local_any), (1, other_any)):
            slot = 2 * j + parity
            offset = pl.multiple_of(info_ref[2 + GROUP_DEVS + slot], span)
            for part, target in ((0, sk_sc), (1, sv_sc)):
                copies.append(
                    pltpu.make_async_copy(
                        source.at[j, pl.ds(2 * block + part * span, span), :],
                        target.at[pl.ds(offset, span), :],
                        sems.at[2 * slot + part],
                    )
                )
    return copies


def attn_kernel(info_ref, q_ref, lk_ref, lv_ref, ok_ref, ov_ref, la_ref, oa_ref, o_ref,
                m_sc, l_sc, acc_sc, sk_sc, sv_sc, sems):
    step = pl.program_id(0)
    last = pl.num_programs(0) - 1
    rows = q_ref.shape[0]
    tokens = o_ref.shape[0]
    heads = rows // tokens
    block = lk_ref.shape[0]
    span = sk_sc.shape[0] // GROUP_DEVS
    length = info_ref[0]
    first_token = info_ref[1]
    start = info_ref[2 + jnp.minimum(step, last - 1)]

    @pl.when(step == 0)
    def _init():
        for copy in span_copies(info_ref, la_ref, oa_ref, sk_sc, sv_sc, sems, block, span):
            copy.start()
        m_sc[...] = jnp.full(m_sc.shape, NEG_FILL, jnp.float32)
        l_sc[...] = jnp.zeros(l_sc.shape, jnp.float32)
        acc_sc[...] = jnp.zeros(acc_sc.shape, jnp.float32)

    def process(keys, values, allowed):
        s = lax.dot_general(
            q_ref[...], keys, (((1,), (1,)), ((), ())), preferred_element_type=jnp.float32
        )
        if allowed is not None:
            s = jnp.where(allowed, s, NEG_FILL)
        m_prev = m_sc[...]
        m_new = jnp.maximum(m_prev, jnp.max(s, axis=1, keepdims=True))
        m_scaled = m_new * EXP2_SCALE
        alpha = jnp.exp2(m_prev * EXP2_SCALE - m_scaled)
        p = jnp.exp2(s * EXP2_SCALE - m_scaled)
        ones = (lax.broadcasted_iota(jnp.int32, values.shape, 1) == 0).astype(values.dtype)
        wide = jnp.concatenate([values, ones], 1)
        pv = jnp.dot(p.astype(jnp.bfloat16), wide, preferred_element_type=jnp.float32)
        l_sc[...] = alpha * l_sc[...] + pv[:, HEAD_SIZE:HEAD_SIZE + 1]
        acc_sc[...] = alpha * acc_sc[...] + pv[:, :HEAD_SIZE]
        m_sc[...] = m_new

    def slot(k_ref, v_ref):
        full = start + block <= length
        partial = jnp.logical_and(start < length, jnp.logical_not(full))

        @pl.when(full)
        def _():
            process(k_ref[...], v_ref[...], None)

        @pl.when(partial)
        def _():
            key_rows = start + lax.broadcasted_iota(jnp.int32, (rows, block), 1)
            process(k_ref[...], v_ref[...], key_rows < length)

    @pl.when(jnp.logical_and(step < last, step % 2 == 0))
    def _local():
        slot(lk_ref, lv_ref)

    @pl.when(jnp.logical_and(step < last, step % 2 == 1))
    def _other():
        slot(ok_ref, ov_ref)

    @pl.when(step == last)
    def _span():
        for copy in span_copies(info_ref, la_ref, oa_ref, sk_sc, sv_sc, sems, block, span):
            copy.wait()
        span_rows = sk_sc.shape[0]
        key_pos = lax.broadcasted_iota(jnp.int32, (rows, span_rows), 1)
        query_pos = first_token + lax.rem(lax.broadcasted_iota(jnp.int32, (rows, span_rows), 0), tokens)
        process(sk_sc[...], sv_sc[...], key_pos <= query_pos)

    @pl.when(step == last)
    def _finish():
        for h in range(heads):
            rows_h = slice(h * tokens, (h + 1) * tokens)
            o_ref[:, h * HEAD_SIZE:(h + 1) * HEAD_SIZE] = (
                acc_sc[rows_h, :] / l_sc[rows_h, :]
            ).astype(o_ref.dtype)


def attention(info, q_rows, local, other, block, span, tokens):
    rows = q_rows.shape[0]
    heads = rows // tokens
    width = heads * HEAD_SIZE
    slots = 2 * local.shape[0]

    def views(pick):
        return [
            pl.BlockSpec((None, block, HEAD_SIZE), lambda k, info: (pick(jnp.minimum(k, slots - 1)), 0, 0)),
            pl.BlockSpec((None, block, HEAD_SIZE), lambda k, info: (pick(jnp.minimum(k, slots - 1)), 1, 0)),
        ]

    fixed = lambda k, info: (0, 0)
    in_specs = (
        [pl.BlockSpec((rows, HEAD_SIZE), fixed)]
        + views(lambda k: k // 2)
        + views(lambda k: jnp.maximum(k - 1, 0) // 2)
        + [pl.BlockSpec(memory_space=pl.ANY), pl.BlockSpec(memory_space=pl.ANY)]
    )
    return pl.pallas_call(
        attn_kernel,
        out_shape=jax.ShapeDtypeStruct((tokens, width), jnp.bfloat16),
        grid_spec=pltpu.PrefetchScalarGridSpec(
            num_scalar_prefetch=1,
            grid=(slots + 1,),
            in_specs=in_specs,
            out_specs=pl.BlockSpec((tokens, width), fixed),
            scratch_shapes=[
                pltpu.VMEM((rows, 1), jnp.float32),
                pltpu.VMEM((rows, 1), jnp.float32),
                pltpu.VMEM((rows, HEAD_SIZE), jnp.float32),
                pltpu.VMEM((slots * span, HEAD_SIZE), jnp.bfloat16),
                pltpu.VMEM((slots * span, HEAD_SIZE), jnp.bfloat16),
                pltpu.SemaphoreType.DMA((4 * slots,)),
            ],
        ),
        compiler_params=pltpu.CompilerParams(
            dimension_semantics=("arbitrary",), vmem_limit_bytes=56 * 1024 * 1024
        ),
    )(info, q_rows, local, local, other, other, local, other)


def pack_kernel(k_ref, v_ref, sk_ref, sv_ref, o_ref):
    rows = k_ref.shape[0]
    span = sk_ref.shape[0]
    o_ref[0:rows, :] = k_ref[...]
    o_ref[rows:2 * rows, :] = v_ref[...]
    o_ref[2 * rows:2 * rows + span, :] = sk_ref[...]
    o_ref[2 * rows + span:2 * rows + 2 * span, :] = sv_ref[...]


def make_pack(cache_k, cache_v, span_k, span_v):
    rows = 2 * cache_k.shape[0] + 2 * span_k.shape[0]
    return pl.pallas_call(
        pack_kernel,
        out_shape=jax.ShapeDtypeStruct((rows, HEAD_SIZE), cache_k.dtype),
    )(cache_k, cache_v, span_k, span_v)


def heads_as_rows(queries):
    tokens, width = queries.shape
    heads = width // HEAD_SIZE
    return queries.reshape(tokens, heads, HEAD_SIZE).transpose(1, 0, 2).reshape(heads * tokens, HEAD_SIZE)


def body(queries, span_rotated_keys, span_token_values, cache_keys, prompt_cache_values, lengths):
    tok_rows = queries.shape[0]
    cache_rows = cache_keys.shape[0]
    group_devs = lax.axis_size("req") // lengths.shape[0]
    assert group_devs == GROUP_DEVS
    device = lax.axis_index("req")
    position = device % GROUP_DEVS
    group_length = lax.dynamic_index_in_dim(lengths, device // GROUP_DEVS, 0, keepdims=False)

    pack = make_pack(cache_keys, prompt_cache_values, span_rotated_keys, span_token_values)
    local, other = gather_group(pack)
    slot_pos = jnp.arange(GROUP_DEVS, dtype=jnp.int32) ^ position
    span_rows = span_rotated_keys.shape[0]
    info = jnp.concatenate(
        [
            jnp.stack([group_length, position * tok_rows]).astype(jnp.int32),
            (slot_pos * cache_rows).astype(jnp.int32),
            (slot_pos * span_rows).astype(jnp.int32),
        ]
    )
    attended = attention(info, heads_as_rows(queries), local, other, cache_rows, span_rows, tok_rows)
    return lax.all_to_all(attended, "tp", split_axis=0, concat_axis=1, tiled=True)


def solution(mesh):
    in_specs = (P("req", "tp"), P("req", "tp"), P("req", "tp"), P("req", "tp"), P("req", "tp"), P())
    out_specs = P(("req", "tp"), None)
    return jax.shard_map(body, mesh=mesh, in_specs=in_specs, out_specs=out_specs, check_vma=False)
```

```python
import functools
import math

import jax
import jax.numpy as jnp
from jax import lax
from jax.experimental import pallas as pl
from jax.experimental.pallas import tpu as pltpu
from jax.sharding import PartitionSpec as P


HEAD_SIZE = 128
GROUP_DEVS = 8
NEG_FILL = -1e30
SCALE = 1.0 / math.sqrt(HEAD_SIZE)
EXP2_SCALE = SCALE * math.log2(math.e)


def exchange(value, axis, mask):
    pairs = [(source, source ^ mask) for source in range(lax.axis_size(axis))]
    return lax.ppermute(value, axis, pairs)


def span_copies(info_ref, local_any, other_any, sk_sc, sv_sc, sems, block, span):
    copies = []
    for j in range(local_any.shape[0]):
        for parity, source in ((0, local_any), (1, other_any)):
            slot = 2 * j + parity
            offset = pl.multiple_of(info_ref[2 + GROUP_DEVS + slot], span)
            for part, target in ((0, sk_sc), (1, sv_sc)):
                copies.append(
                    pltpu.make_async_copy(
                        source.at[j, pl.ds(2 * block + part * span, span), :],
                        target.at[pl.ds(offset, span), :],
                        sems.at[2 * slot + part],
                    )
                )
    return copies


def attn_kernel(plan, first, final, info_ref, q_ref, *refs):
    refs = list(refs)
    n_arrays = max(array for array, _ in plan) + 1
    state_in = [] if first else [refs.pop(0) for _ in range(3)]
    kv_refs = [(refs.pop(0), refs.pop(0)) for _ in range(n_arrays)]
    if final:
        la_ref, oa_ref, o_ref = refs.pop(0), refs.pop(0), refs.pop(0)
        m_sc, l_sc, acc_sc, sk_sc, sv_sc, sems = refs
    else:
        m_out, l_out, acc_out, m_sc, l_sc, acc_sc = refs
    step = pl.program_id(0)
    last = pl.num_programs(0) - 1
    rows = q_ref.shape[0]
    block = kv_refs[0][0].shape[0]
    length = info_ref[0]
    first_token = info_ref[1]

    @pl.when(step == 0)
    def _init():
        if final:
            span = sk_sc.shape[0] // GROUP_DEVS
            for copy in span_copies(info_ref, la_ref, oa_ref, sk_sc, sv_sc, sems, block, span):
                copy.start()
        if first:
            m_sc[...] = jnp.full(m_sc.shape, NEG_FILL, jnp.float32)
            l_sc[...] = jnp.zeros(l_sc.shape, jnp.float32)
            acc_sc[...] = jnp.zeros(acc_sc.shape, jnp.float32)
        else:
            m_sc[...] = state_in[0][...]
            l_sc[...] = state_in[1][...]
            acc_sc[...] = state_in[2][...]

    def process(keys, values, allowed):
        s = lax.dot_general(
            q_ref[...], keys, (((1,), (1,)), ((), ())), preferred_element_type=jnp.float32
        )
        if allowed is not None:
            s = jnp.where(allowed, s, NEG_FILL)
        m_prev = m_sc[...]
        m_new = jnp.maximum(m_prev, jnp.max(s, axis=1, keepdims=True))
        alpha = jnp.exp2((m_prev - m_new) * EXP2_SCALE)
        p = jnp.exp2((s - m_new) * EXP2_SCALE)
        l_sc[...] = alpha * l_sc[...] + jnp.sum(p, axis=1, keepdims=True)
        pv = jnp.dot(p.astype(jnp.bfloat16), values, preferred_element_type=jnp.float32)
        acc_sc[...] = alpha * acc_sc[...] + pv
        m_sc[...] = m_new

    def slot(k_ref, v_ref, start):
        full = start + block <= length
        partial = jnp.logical_and(start < length, jnp.logical_not(full))

        @pl.when(full)
        def _():
            process(k_ref[...], v_ref[...], None)

        @pl.when(partial)
        def _():
            key_rows = start + lax.broadcasted_iota(jnp.int32, (rows, block), 1)
            process(k_ref[...], v_ref[...], key_rows < length)

    for array in range(n_arrays):
        steps = [i for i, (a, _) in enumerate(plan) if a == array]
        uses = functools.reduce(jnp.logical_or, [step == i for i in steps])

        @pl.when(uses)
        def _():
            slot(kv_refs[array][0], kv_refs[array][1], info_ref[2 + 2 * GROUP_DEVS + step])

    if final:
        tokens = o_ref.shape[0]
        heads = rows // tokens

        @pl.when(step == last)
        def _span():
            span = sk_sc.shape[0] // GROUP_DEVS
            for copy in span_copies(info_ref, la_ref, oa_ref, sk_sc, sv_sc, sems, block, span):
                copy.wait()
            span_rows = sk_sc.shape[0]
            key_pos = lax.broadcasted_iota(jnp.int32, (rows, span_rows), 1)
            query_pos = first_token + lax.rem(
                lax.broadcasted_iota(jnp.int32, (rows, span_rows), 0), tokens
            )
            process(sk_sc[...], sv_sc[...], key_pos <= query_pos)
            for h in range(heads):
                rows_h = slice(h * tokens, (h + 1) * tokens)
                o_ref[:, h * HEAD_SIZE:(h + 1) * HEAD_SIZE] = (
                    acc_sc[rows_h, :] / l_sc[rows_h, :]
                ).astype(o_ref.dtype)
    else:
        @pl.when(step == last)
        def _save():
            m_out[...] = m_sc[...]
            l_out[...] = l_sc[...]
            acc_out[...] = acc_sc[...]


def index_map(plan, array):
    used = [(i, index) for i, (a, index) in enumerate(plan) if a == array]
    table = []
    for i in range(len(plan) + 1):
        before = [index for j, index in used if j <= i]
        table.append(before[-1] if before else used[0][1])

    def pick(k):
        result = table[-1]
        for i in reversed(range(len(table) - 1)):
            result = jnp.where(k == i, table[i], result)
        return result

    return pick


def attention(info, q_rows, arrays, plan, state, span_sources, tokens, block, span):
    rows = q_rows.shape[0]
    first = state is None
    final = span_sources is not None
    n_steps = len(plan) + (1 if final else 0)
    fixed = lambda k, info: (0, 0)
    in_specs = [pl.BlockSpec((rows, HEAD_SIZE), fixed)]
    operands = [info, q_rows]
    if not first:
        in_specs += [pl.BlockSpec((rows, 1), fixed), pl.BlockSpec((rows, 1), fixed),
                     pl.BlockSpec((rows, HEAD_SIZE), fixed)]
        operands += list(state)
    for array_id, array in enumerate(arrays):
        pick = index_map(plan, array_id)
        in_specs += [
            pl.BlockSpec((None, block, HEAD_SIZE), lambda k, info, pick=pick: (pick(k), 0, 0)),
            pl.BlockSpec((None, block, HEAD_SIZE), lambda k, info, pick=pick: (pick(k), 1, 0)),
        ]
        operands += [array, array]
    scratch = [
        pltpu.VMEM((rows, 1), jnp.float32),
        pltpu.VMEM((rows, 1), jnp.float32),
        pltpu.VMEM((rows, HEAD_SIZE), jnp.float32),
    ]
    if final:
        in_specs += [pl.BlockSpec(memory_space=pl.ANY), pl.BlockSpec(memory_space=pl.ANY)]
        operands += list(span_sources)
        heads = rows // tokens
        out_shape = jax.ShapeDtypeStruct((tokens, heads * HEAD_SIZE), jnp.bfloat16)
        out_specs = pl.BlockSpec((tokens, heads * HEAD_SIZE), fixed)
        scratch += [
            pltpu.VMEM((GROUP_DEVS * span, HEAD_SIZE), jnp.bfloat16),
            pltpu.VMEM((GROUP_DEVS * span, HEAD_SIZE), jnp.bfloat16),
            pltpu.SemaphoreType.DMA((4 * GROUP_DEVS,)),
        ]
    else:
        out_shape = (
            jax.ShapeDtypeStruct((rows, 1), jnp.float32),
            jax.ShapeDtypeStruct((rows, 1), jnp.float32),
            jax.ShapeDtypeStruct((rows, HEAD_SIZE), jnp.float32),
        )
        out_specs = (pl.BlockSpec((rows, 1), fixed), pl.BlockSpec((rows, 1), fixed),
                     pl.BlockSpec((rows, HEAD_SIZE), fixed))
    flops = 4 * rows * block * HEAD_SIZE * n_steps
    return pl.pallas_call(
        functools.partial(attn_kernel, plan, first, final),
        out_shape=out_shape,
        grid_spec=pltpu.PrefetchScalarGridSpec(
            num_scalar_prefetch=1,
            grid=(n_steps,),
            in_specs=in_specs,
            out_specs=out_specs,
            scratch_shapes=scratch,
        ),
        compiler_params=pltpu.CompilerParams(
            dimension_semantics=("arbitrary",), vmem_limit_bytes=56 * 1024 * 1024
        ),
        cost_estimate=pl.CostEstimate(
            flops=flops, transcendentals=rows * block * n_steps,
            bytes_accessed=n_steps * 2 * block * HEAD_SIZE * 2,
        ),
    )(*operands)


def pack_kernel(k_ref, v_ref, sk_ref, sv_ref, o_ref):
    rows = k_ref.shape[0]
    span = sk_ref.shape[0]
    o_ref[0:rows, :] = k_ref[...]
    o_ref[rows:2 * rows, :] = v_ref[...]
    o_ref[2 * rows:2 * rows + span, :] = sk_ref[...]
    o_ref[2 * rows + span:2 * rows + 2 * span, :] = sv_ref[...]


def make_pack(cache_k, cache_v, span_k, span_v):
    rows = 2 * cache_k.shape[0] + 2 * span_k.shape[0]
    return pl.pallas_call(
        pack_kernel,
        out_shape=jax.ShapeDtypeStruct((rows, HEAD_SIZE), cache_k.dtype),
    )(cache_k, cache_v, span_k, span_v)


def heads_as_rows(queries):
    tokens, width = queries.shape
    heads = width // HEAD_SIZE
    return queries.reshape(tokens, heads, HEAD_SIZE).transpose(1, 0, 2).reshape(heads * tokens, HEAD_SIZE)


def body(queries, span_rotated_keys, span_token_values, cache_keys, prompt_cache_values, lengths):
    tok_rows = queries.shape[0]
    cache_rows = cache_keys.shape[0]
    group_devs = lax.axis_size("req") // lengths.shape[0]
    assert group_devs == GROUP_DEVS
    device = lax.axis_index("req")
    position = device % GROUP_DEVS
    group_length = lax.dynamic_index_in_dim(lengths, device // GROUP_DEVS, 0, keepdims=False)

    pack = make_pack(cache_keys, prompt_cache_values, span_rotated_keys, span_token_values)
    span_rows = span_rotated_keys.shape[0]
    slot_pos = jnp.arange(GROUP_DEVS, dtype=jnp.int32) ^ position
    starts = slot_pos * cache_rows
    step_slots = jnp.asarray([0, 2, 4, 6, 1, 3, 5, 7], jnp.int32)
    info = jnp.concatenate(
        [
            jnp.stack([group_length, position * tok_rows]).astype(jnp.int32),
            starts.astype(jnp.int32),
            (slot_pos * span_rows).astype(jnp.int32),
            starts[step_slots].astype(jnp.int32),
        ]
    )
    info_b = jnp.concatenate([info[:2 + 2 * GROUP_DEVS], info[2 + 2 * GROUP_DEVS + 1:]])
    info_c = jnp.concatenate([info[:2 + 2 * GROUP_DEVS], info[2 + 2 * GROUP_DEVS + 3:]])
    q_rows = heads_as_rows(queries)
    size = (tok_rows, cache_rows, span_rows)

    half = pack.shape[0] // 2
    from_x = exchange(pack, "req", 2)
    from_z = exchange(pack, "req", 4)
    state = attention(info, q_rows, [pack[None]], [(0, 0)], None, None, *size)
    diag_lo = exchange(from_z[:half], "req", 2)
    diag_hi = exchange(from_x[half:], "req", 4)
    state = attention(
        info_b, q_rows, [from_x[None], from_z[None]], [(0, 0), (1, 0)], state, None, *size
    )
    diag = jnp.concatenate([diag_lo, diag_hi], 0)
    local = jnp.stack([pack, from_x, from_z, diag])
    other = exchange(local, "req", 1)
    plan = [(0, 3), (1, 0), (1, 1), (1, 2), (1, 3)]
    attended = attention(info_c, q_rows, [local, other], plan, state, (local, other), *size)
    return lax.all_to_all(attended, "tp", split_axis=0, concat_axis=1, tiled=True)


def solution(mesh):
    in_specs = (P("req", "tp"), P("req", "tp"), P("req", "tp"), P("req", "tp"), P("req", "tp"), P())
    out_specs = P(("req", "tp"), None)
    return jax.shard_map(body, mesh=mesh, in_specs=in_specs, out_specs=out_specs, check_vma=False)
```

```python
import functools
import math

import jax
import jax.numpy as jnp
from jax import lax
from jax.experimental import pallas as pl
from jax.experimental.pallas import tpu as pltpu
from jax.sharding import PartitionSpec as P


HEAD_SIZE = 128
GROUP_DEVS = 8
STEP_SLOTS = (0, 2, 4, 6, 1, 3, 5, 7)
NEG_FILL = -1e30
SCALE = 1.0 / math.sqrt(HEAD_SIZE)
EXP2_SCALE = SCALE * math.log2(math.e)


def exchange(value, axis, mask):
    pairs = [(source, source ^ mask) for source in range(lax.axis_size(axis))]
    return lax.ppermute(value, axis, pairs)


def span_copies(info_ref, local_any, other_any, sk_sc, sv_sc, sems, block, span):
    copies = []
    for j in range(local_any.shape[0]):
        for parity, source in ((0, local_any), (1, other_any)):
            slot = 2 * j + parity
            offset = pl.multiple_of(info_ref[2 + GROUP_DEVS + slot], span)
            for part, target in ((0, sk_sc), (1, sv_sc)):
                copies.append(
                    pltpu.make_async_copy(
                        source.at[j, pl.ds(2 * block + part * span, span), :],
                        target.at[pl.ds(offset, span), :],
                        sems.at[2 * slot + part],
                    )
                )
    return copies


def attn_kernel(plan, offset, first, final, info_ref, q_ref, *refs):
    refs = list(refs)
    n_arrays = max(array for array, _ in plan) + 1
    state_in = [] if first else [refs.pop(0) for _ in range(3)]
    kv_refs = [(refs.pop(0), refs.pop(0)) for _ in range(n_arrays)]
    if final:
        la_ref, oa_ref, o_ref = refs.pop(0), refs.pop(0), refs.pop(0)
        m_sc, l_sc, acc_sc, sk_sc, sv_sc, sems = refs
    else:
        m_out, l_out, acc_out, m_sc, l_sc, acc_sc = refs
    step = pl.program_id(0)
    last = pl.num_programs(0) - 1
    rows = q_ref.shape[0]
    block = kv_refs[0][0].shape[0]
    length = info_ref[0]
    first_token = info_ref[1]

    @pl.when(step == 0)
    def _init():
        if final:
            span = sk_sc.shape[0] // GROUP_DEVS
            for copy in span_copies(info_ref, la_ref, oa_ref, sk_sc, sv_sc, sems, block, span):
                copy.start()
        if first:
            m_sc[...] = jnp.full(m_sc.shape, NEG_FILL, jnp.float32)
            l_sc[...] = jnp.zeros(l_sc.shape, jnp.float32)
            acc_sc[...] = jnp.zeros(acc_sc.shape, jnp.float32)
        else:
            m_sc[...] = state_in[0][...]
            l_sc[...] = state_in[1][...]
            acc_sc[...] = state_in[2][...]

    def process(keys, values, allowed):
        s = lax.dot_general(
            q_ref[...], keys, (((1,), (1,)), ((), ())), preferred_element_type=jnp.float32
        )
        if allowed is not None:
            s = jnp.where(allowed, s, NEG_FILL)
        m_prev = m_sc[...]
        m_new = jnp.maximum(m_prev, jnp.max(s, axis=1, keepdims=True))
        alpha = jnp.exp2((m_prev - m_new) * EXP2_SCALE)
        p = jnp.exp2((s - m_new) * EXP2_SCALE)
        l_sc[...] = alpha * l_sc[...] + jnp.sum(p, axis=1, keepdims=True)
        pv = jnp.dot(p.astype(jnp.bfloat16), values, preferred_element_type=jnp.float32)
        acc_sc[...] = alpha * acc_sc[...] + pv
        m_sc[...] = m_new

    def slot(k_ref, v_ref, start):
        full = start + block <= length
        partial = jnp.logical_and(start < length, jnp.logical_not(full))

        @pl.when(full)
        def _():
            process(k_ref[...], v_ref[...], None)

        @pl.when(partial)
        def _():
            key_rows = start + lax.broadcasted_iota(jnp.int32, (rows, block), 1)
            process(k_ref[...], v_ref[...], key_rows < length)

    for array in range(n_arrays):
        steps = [i for i, (a, _) in enumerate(plan) if a == array]
        uses = functools.reduce(jnp.logical_or, [step == i for i in steps])

        @pl.when(uses)
        def _():
            slot(kv_refs[array][0], kv_refs[array][1], info_ref[2 + 2 * GROUP_DEVS + offset + step])

    if final:
        tokens = o_ref.shape[0]
        heads = rows // tokens

        @pl.when(step == last)
        def _span():
            span = sk_sc.shape[0] // GROUP_DEVS
            for copy in span_copies(info_ref, la_ref, oa_ref, sk_sc, sv_sc, sems, block, span):
                copy.wait()
            span_rows = sk_sc.shape[0]
            key_pos = lax.broadcasted_iota(jnp.int32, (rows, span_rows), 1)
            query_pos = first_token + lax.rem(
                lax.broadcasted_iota(jnp.int32, (rows, span_rows), 0), tokens
            )
            process(sk_sc[...], sv_sc[...], key_pos <= query_pos)
            for h in range(heads):
                rows_h = slice(h * tokens, (h + 1) * tokens)
                o_ref[:, h * HEAD_SIZE:(h + 1) * HEAD_SIZE] = (
                    acc_sc[rows_h, :] / l_sc[rows_h, :]
                ).astype(o_ref.dtype)
    else:
        @pl.when(step == last)
        def _save():
            m_out[...] = m_sc[...]
            l_out[...] = l_sc[...]
            acc_out[...] = acc_sc[...]


def index_map(plan, array):
    used = [(i, index) for i, (a, index) in enumerate(plan) if a == array]
    table = []
    for i in range(len(plan) + 1):
        before = [index for j, index in used if j <= i]
        table.append(before[-1] if before else used[0][1])

    def pick(k):
        result = table[-1]
        for i in reversed(range(len(table) - 1)):
            result = jnp.where(k == i, table[i], result)
        return result

    return pick


def attention(info, offset, q_rows, arrays, plan, state, span_sources, tokens, block, span):
    rows = q_rows.shape[0]
    first = state is None
    final = span_sources is not None
    n_steps = len(plan) + (1 if final else 0)
    fixed = lambda k, info: (0, 0)
    in_specs = [pl.BlockSpec((rows, HEAD_SIZE), fixed)]
    operands = [info, q_rows]
    if not first:
        in_specs += [pl.BlockSpec((rows, 1), fixed), pl.BlockSpec((rows, 1), fixed),
                     pl.BlockSpec((rows, HEAD_SIZE), fixed)]
        operands += list(state)
    for array_id, array in enumerate(arrays):
        pick = index_map(plan, array_id)
        in_specs += [
            pl.BlockSpec((None, block, HEAD_SIZE), lambda k, info, pick=pick: (pick(k), 0, 0)),
            pl.BlockSpec((None, block, HEAD_SIZE), lambda k, info, pick=pick: (pick(k), 1, 0)),
        ]
        operands += [array, array]
    scratch = [
        pltpu.VMEM((rows, 1), jnp.float32),
        pltpu.VMEM((rows, 1), jnp.float32),
        pltpu.VMEM((rows, HEAD_SIZE), jnp.float32),
    ]
    if final:
        in_specs += [pl.BlockSpec(memory_space=pl.ANY), pl.BlockSpec(memory_space=pl.ANY)]
        operands += list(span_sources)
        heads = rows // tokens
        out_shape = jax.ShapeDtypeStruct((tokens, heads * HEAD_SIZE), jnp.bfloat16)
        out_specs = pl.BlockSpec((tokens, heads * HEAD_SIZE), fixed)
        scratch += [
            pltpu.VMEM((GROUP_DEVS * span, HEAD_SIZE), jnp.bfloat16),
            pltpu.VMEM((GROUP_DEVS * span, HEAD_SIZE), jnp.bfloat16),
            pltpu.SemaphoreType.DMA((4 * GROUP_DEVS,)),
        ]
    else:
        out_shape = (
            jax.ShapeDtypeStruct((rows, 1), jnp.float32),
            jax.ShapeDtypeStruct((rows, 1), jnp.float32),
            jax.ShapeDtypeStruct((rows, HEAD_SIZE), jnp.float32),
        )
        out_specs = (pl.BlockSpec((rows, 1), fixed), pl.BlockSpec((rows, 1), fixed),
                     pl.BlockSpec((rows, HEAD_SIZE), fixed))
    flops = 4 * rows * block * HEAD_SIZE * n_steps
    return pl.pallas_call(
        functools.partial(attn_kernel, plan, offset, first, final),
        out_shape=out_shape,
        grid_spec=pltpu.PrefetchScalarGridSpec(
            num_scalar_prefetch=1,
            grid=(n_steps,),
            in_specs=in_specs,
            out_specs=out_specs,
            scratch_shapes=scratch,
        ),
        compiler_params=pltpu.CompilerParams(
            dimension_semantics=("arbitrary",), vmem_limit_bytes=56 * 1024 * 1024
        ),
        cost_estimate=pl.CostEstimate(
            flops=flops, transcendentals=rows * block * n_steps,
            bytes_accessed=n_steps * 2 * block * HEAD_SIZE * 2,
        ),
    )(*operands)


def pack_kernel(k_ref, v_ref, sk_ref, sv_ref, o_ref):
    rows = k_ref.shape[0]
    span = sk_ref.shape[0]
    o_ref[0:rows, :] = k_ref[...]
    o_ref[rows:2 * rows, :] = v_ref[...]
    o_ref[2 * rows:2 * rows + span, :] = sk_ref[...]
    o_ref[2 * rows + span:2 * rows + 2 * span, :] = sv_ref[...]


def make_pack(cache_k, cache_v, span_k, span_v):
    rows = 2 * cache_k.shape[0] + 2 * span_k.shape[0]
    return pl.pallas_call(
        pack_kernel,
        out_shape=jax.ShapeDtypeStruct((rows, HEAD_SIZE), cache_k.dtype),
    )(cache_k, cache_v, span_k, span_v)


def heads_as_rows(queries):
    tokens, width = queries.shape
    heads = width // HEAD_SIZE
    return queries.reshape(tokens, heads, HEAD_SIZE).transpose(1, 0, 2).reshape(heads * tokens, HEAD_SIZE)


def body(queries, span_rotated_keys, span_token_values, cache_keys, prompt_cache_values, lengths):
    tok_rows = queries.shape[0]
    cache_rows = cache_keys.shape[0]
    group_devs = lax.axis_size("req") // lengths.shape[0]
    assert group_devs == GROUP_DEVS
    device = lax.axis_index("req")
    position = device % GROUP_DEVS
    group_length = lax.dynamic_index_in_dim(lengths, device // GROUP_DEVS, 0, keepdims=False)

    pack = make_pack(cache_keys, prompt_cache_values, span_rotated_keys, span_token_values)
    span_rows = span_rotated_keys.shape[0]
    slot_pos = jnp.arange(GROUP_DEVS, dtype=jnp.int32) ^ position
    step_pos = jnp.asarray(STEP_SLOTS, jnp.int32) ^ position
    info = jnp.concatenate(
        [
            jnp.stack([group_length, position * tok_rows]).astype(jnp.int32),
            (slot_pos * cache_rows).astype(jnp.int32),
            (slot_pos * span_rows).astype(jnp.int32),
            (step_pos * cache_rows).astype(jnp.int32),
        ]
    )
    q_rows = heads_as_rows(queries)
    size = (tok_rows, cache_rows, span_rows)

    half = pack.shape[0] // 2
    from_x = exchange(pack, "req", 2)
    from_z = exchange(pack, "req", 4)
    state = attention(info, 0, q_rows, [pack[None]], [(0, 0)], None, None, *size)
    diag_lo = exchange(from_z[:half], "req", 2)
    diag_hi = exchange(from_x[half:], "req", 4)
    state = attention(
        info, 1, q_rows, [from_x[None], from_z[None]], [(0, 0), (1, 0)], state, None, *size
    )
    diag = jnp.concatenate([diag_lo, diag_hi], 0)
    local = jnp.stack([pack, from_x, from_z, diag])
    other = exchange(local, "req", 1)
    plan = [(0, 3), (1, 0), (1, 1), (1, 2), (1, 3)]
    attended = attention(info, 3, q_rows, [local, other], plan, state, (local, other), *size)
    return lax.all_to_all(attended, "tp", split_axis=0, concat_axis=1, tiled=True)


def solution(mesh):
    in_specs = (P("req", "tp"), P("req", "tp"), P("req", "tp"), P("req", "tp"), P("req", "tp"), P())
    out_specs = P(("req", "tp"), None)
    return jax.shard_map(body, mesh=mesh, in_specs=in_specs, out_specs=out_specs, check_vma=False)
```

```python
import functools
import math

import jax
import jax.numpy as jnp
from jax import lax
from jax.experimental import pallas as pl
from jax.experimental.pallas import tpu as pltpu
from jax.sharding import PartitionSpec as P


HEAD_SIZE = 128
GROUP_DEVS = 8
STEP_SLOTS = (0, 2, 4, 6, 1, 3, 5, 7)
NEG_FILL = -1e30
SCALE = 1.0 / math.sqrt(HEAD_SIZE)
EXP2_SCALE = SCALE * math.log2(math.e)


def exchange(value, axis, mask):
    pairs = [(source, source ^ mask) for source in range(lax.axis_size(axis))]
    return lax.ppermute(value, axis, pairs)


def span_copies(info_ref, sources, plan, sk_sc, sv_sc, sems, block, span):
    copies = []
    for source_id, j, slot in plan:
        offset = pl.multiple_of(info_ref[2 + GROUP_DEVS + slot], span)
        for part, target in ((0, sk_sc), (1, sv_sc)):
            copies.append(
                pltpu.make_async_copy(
                    sources[source_id].at[j, pl.ds(2 * block + part * span, span), :],
                    target.at[pl.ds(offset, span), :],
                    sems.at[2 * slot + part],
                )
            )
    return copies


def attn_kernel(plan, offset, first, final, span_plan, info_ref, q_ref, *refs):
    refs = list(refs)
    n_arrays = max(array for array, _ in plan) + 1
    state_in = [] if first else [refs.pop(0) for _ in range(3)]
    kv_refs = [(refs.pop(0), refs.pop(0)) for _ in range(n_arrays)]
    if final:
        n_sources = max(source for source, _, _ in span_plan) + 1
        span_refs = [refs.pop(0) for _ in range(n_sources)]
        o_ref = refs.pop(0)
        m_sc, l_sc, acc_sc, sk_sc, sv_sc, sems = refs
    else:
        m_out, l_out, acc_out, m_sc, l_sc, acc_sc = refs
    step = pl.program_id(0)
    last = pl.num_programs(0) - 1
    rows = q_ref.shape[0]
    block = kv_refs[0][0].shape[0]
    length = info_ref[0]
    first_token = info_ref[1]

    @pl.when(step == 0)
    def _init():
        if final:
            span = sk_sc.shape[0] // GROUP_DEVS
            for copy in span_copies(info_ref, span_refs, span_plan, sk_sc, sv_sc, sems, block, span):
                copy.start()
        if first:
            m_sc[...] = jnp.full(m_sc.shape, NEG_FILL, jnp.float32)
            l_sc[...] = jnp.zeros(l_sc.shape, jnp.float32)
            acc_sc[...] = jnp.zeros(acc_sc.shape, jnp.float32)
        else:
            m_sc[...] = state_in[0][...]
            l_sc[...] = state_in[1][...]
            acc_sc[...] = state_in[2][...]

    def process(keys, values, allowed):
        s = lax.dot_general(
            q_ref[...], keys, (((1,), (1,)), ((), ())), preferred_element_type=jnp.float32
        )
        if allowed is not None:
            s = jnp.where(allowed, s, NEG_FILL)
        m_prev = m_sc[...]
        m_new = jnp.maximum(m_prev, jnp.max(s, axis=1, keepdims=True))
        alpha = jnp.exp2((m_prev - m_new) * EXP2_SCALE)
        p = jnp.exp2((s - m_new) * EXP2_SCALE)
        l_sc[...] = alpha * l_sc[...] + jnp.sum(p, axis=1, keepdims=True)
        pv = jnp.dot(p.astype(jnp.bfloat16), values, preferred_element_type=jnp.float32)
        acc_sc[...] = alpha * acc_sc[...] + pv
        m_sc[...] = m_new

    def slot(k_ref, v_ref, start):
        full = start + block <= length
        partial = jnp.logical_and(start < length, jnp.logical_not(full))

        @pl.when(full)
        def _():
            process(k_ref[...], v_ref[...], None)

        @pl.when(partial)
        def _():
            key_rows = start + lax.broadcasted_iota(jnp.int32, (rows, block), 1)
            process(k_ref[...], v_ref[...], key_rows < length)

    for array in range(n_arrays):
        steps = [i for i, (a, _) in enumerate(plan) if a == array]
        uses = functools.reduce(jnp.logical_or, [step == i for i in steps])

        @pl.when(uses)
        def _():
            slot(kv_refs[array][0], kv_refs[array][1], info_ref[2 + 2 * GROUP_DEVS + offset + step])

    if final:
        tokens = o_ref.shape[0]
        heads = rows // tokens

        @pl.when(step == last)
        def _span():
            span = sk_sc.shape[0] // GROUP_DEVS
            for copy in span_copies(info_ref, span_refs, span_plan, sk_sc, sv_sc, sems, block, span):
                copy.wait()
            span_rows = sk_sc.shape[0]
            key_pos = lax.broadcasted_iota(jnp.int32, (rows, span_rows), 1)
            query_pos = first_token + lax.rem(
                lax.broadcasted_iota(jnp.int32, (rows, span_rows), 0), tokens
            )
            process(sk_sc[...], sv_sc[...], key_pos <= query_pos)
            for h in range(heads):
                rows_h = slice(h * tokens, (h + 1) * tokens)
                o_ref[:, h * HEAD_SIZE:(h + 1) * HEAD_SIZE] = (
                    acc_sc[rows_h, :] / l_sc[rows_h, :]
                ).astype(o_ref.dtype)
    else:
        @pl.when(step == last)
        def _save():
            m_out[...] = m_sc[...]
            l_out[...] = l_sc[...]
            acc_out[...] = acc_sc[...]


def index_map(plan, array):
    used = [(i, index) for i, (a, index) in enumerate(plan) if a == array]
    table = []
    for i in range(len(plan) + 1):
        before = [index for j, index in used if j <= i]
        table.append(before[-1] if before else used[0][1])

    def pick(k):
        result = table[-1]
        for i in reversed(range(len(table) - 1)):
            result = jnp.where(k == i, table[i], result)
        return result

    return pick


def attention(info, offset, q_rows, arrays, plan, state, span_sources, tokens, block, span,
              span_plan=None):
    rows = q_rows.shape[0]
    first = state is None
    final = span_sources is not None
    n_steps = len(plan) + (1 if final else 0)
    fixed = lambda k, info: (0, 0)
    in_specs = [pl.BlockSpec((rows, HEAD_SIZE), fixed)]
    operands = [info, q_rows]
    if not first:
        in_specs += [pl.BlockSpec((rows, 1), fixed), pl.BlockSpec((rows, 1), fixed),
                     pl.BlockSpec((rows, HEAD_SIZE), fixed)]
        operands += list(state)
    for array_id, array in enumerate(arrays):
        pick = index_map(plan, array_id)
        in_specs += [
            pl.BlockSpec((None, block, HEAD_SIZE), lambda k, info, pick=pick: (pick(k), 0, 0)),
            pl.BlockSpec((None, block, HEAD_SIZE), lambda k, info, pick=pick: (pick(k), 1, 0)),
        ]
        operands += [array, array]
    scratch = [
        pltpu.VMEM((rows, 1), jnp.float32),
        pltpu.VMEM((rows, 1), jnp.float32),
        pltpu.VMEM((rows, HEAD_SIZE), jnp.float32),
    ]
    if final:
        in_specs += [pl.BlockSpec(memory_space=pl.ANY) for _ in span_sources]
        operands += list(span_sources)
        heads = rows // tokens
        out_shape = jax.ShapeDtypeStruct((tokens, heads * HEAD_SIZE), jnp.bfloat16)
        out_specs = pl.BlockSpec((tokens, heads * HEAD_SIZE), fixed)
        scratch += [
            pltpu.VMEM((GROUP_DEVS * span, HEAD_SIZE), jnp.bfloat16),
            pltpu.VMEM((GROUP_DEVS * span, HEAD_SIZE), jnp.bfloat16),
            pltpu.SemaphoreType.DMA((4 * GROUP_DEVS,)),
        ]
    else:
        out_shape = (
            jax.ShapeDtypeStruct((rows, 1), jnp.float32),
            jax.ShapeDtypeStruct((rows, 1), jnp.float32),
            jax.ShapeDtypeStruct((rows, HEAD_SIZE), jnp.float32),
        )
        out_specs = (pl.BlockSpec((rows, 1), fixed), pl.BlockSpec((rows, 1), fixed),
                     pl.BlockSpec((rows, HEAD_SIZE), fixed))
    flops = 4 * rows * block * HEAD_SIZE * n_steps
    return pl.pallas_call(
        functools.partial(attn_kernel, plan, offset, first, final, span_plan),
        out_shape=out_shape,
        grid_spec=pltpu.PrefetchScalarGridSpec(
            num_scalar_prefetch=1,
            grid=(n_steps,),
            in_specs=in_specs,
            out_specs=out_specs,
            scratch_shapes=scratch,
        ),
        compiler_params=pltpu.CompilerParams(
            dimension_semantics=("arbitrary",), vmem_limit_bytes=56 * 1024 * 1024
        ),
        cost_estimate=pl.CostEstimate(
            flops=flops, transcendentals=rows * block * n_steps,
            bytes_accessed=n_steps * 2 * block * HEAD_SIZE * 2,
        ),
    )(*operands)


def pack_kernel(k_ref, v_ref, sk_ref, sv_ref, o_ref):
    rows = k_ref.shape[0]
    span = sk_ref.shape[0]
    o_ref[0:rows, :] = k_ref[...]
    o_ref[rows:2 * rows, :] = v_ref[...]
    o_ref[2 * rows:2 * rows + span, :] = sk_ref[...]
    o_ref[2 * rows + span:2 * rows + 2 * span, :] = sv_ref[...]


def make_pack(cache_k, cache_v, span_k, span_v):
    rows = 2 * cache_k.shape[0] + 2 * span_k.shape[0]
    return pl.pallas_call(
        pack_kernel,
        out_shape=jax.ShapeDtypeStruct((rows, HEAD_SIZE), cache_k.dtype),
    )(cache_k, cache_v, span_k, span_v)


def heads_as_rows(queries):
    tokens, width = queries.shape
    heads = width // HEAD_SIZE
    return queries.reshape(tokens, heads, HEAD_SIZE).transpose(1, 0, 2).reshape(heads * tokens, HEAD_SIZE)


def body(queries, span_rotated_keys, span_token_values, cache_keys, prompt_cache_values, lengths):
    tok_rows = queries.shape[0]
    cache_rows = cache_keys.shape[0]
    group_devs = lax.axis_size("req") // lengths.shape[0]
    assert group_devs == GROUP_DEVS
    device = lax.axis_index("req")
    position = device % GROUP_DEVS
    group_length = lax.dynamic_index_in_dim(lengths, device // GROUP_DEVS, 0, keepdims=False)

    pack = make_pack(cache_keys, prompt_cache_values, span_rotated_keys, span_token_values)
    span_rows = span_rotated_keys.shape[0]
    slot_pos = jnp.arange(GROUP_DEVS, dtype=jnp.int32) ^ position
    step_pos = jnp.asarray(STEP_SLOTS, jnp.int32) ^ position
    info = jnp.concatenate(
        [
            jnp.stack([group_length, position * tok_rows]).astype(jnp.int32),
            (slot_pos * cache_rows).astype(jnp.int32),
            (slot_pos * span_rows).astype(jnp.int32),
            (step_pos * cache_rows).astype(jnp.int32),
        ]
    )
    q_rows = heads_as_rows(queries)
    size = (tok_rows, cache_rows, span_rows)

    half = pack.shape[0] // 2
    from_x = exchange(pack, "req", 2)
    from_z = exchange(pack, "req", 4)
    state = attention(info, 0, q_rows, [pack[None]], [(0, 0)], None, None, *size)
    early = jnp.stack([pack, from_x, from_z])
    diag_lo = exchange(from_z[:half], "req", 2)
    diag_hi = exchange(from_x[half:], "req", 4)
    other_early = exchange(early, "req", 1)
    state = attention(
        info, 1, q_rows, [from_x[None], from_z[None]], [(0, 0), (1, 0)], state, None, *size
    )
    diag = jnp.concatenate([diag_lo, diag_hi], 0)[None]
    other_diag = exchange(diag, "req", 1)
    plan = [(0, 0), (1, 0), (1, 1), (1, 2), (2, 0)]
    span_plan = [(0, 0, 0), (0, 1, 2), (0, 2, 4), (1, 0, 6), (2, 0, 1), (2, 1, 3), (2, 2, 5),
                 (3, 0, 7)]
    attended = attention(
        info, 3, q_rows, [diag, other_early, other_diag], plan, state,
        (early, diag, other_early, other_diag), *size, span_plan=span_plan,
    )
    return lax.all_to_all(attended, "tp", split_axis=0, concat_axis=1, tiled=True)


def solution(mesh):
    in_specs = (P("req", "tp"), P("req", "tp"), P("req", "tp"), P("req", "tp"), P("req", "tp"), P())
    out_specs = P(("req", "tp"), None)
    return jax.shard_map(body, mesh=mesh, in_specs=in_specs, out_specs=out_specs, check_vma=False)
```

```python
import functools
import math

import jax
import jax.numpy as jnp
from jax import lax
from jax.experimental import pallas as pl
from jax.experimental.pallas import tpu as pltpu
from jax.sharding import Mesh, PartitionSpec as P


HEAD_SIZE = 128
GROUP_DEVS = 8
TP_HI = 2
STEP_SLOTS = (0, 2, 4, 6, 1, 3, 5, 7)
NEG_FILL = -1e30
SCALE = 1.0 / math.sqrt(HEAD_SIZE)
EXP2_SCALE = SCALE * math.log2(math.e)


def exchange(value, axis, mask):
    pairs = [(source, source ^ mask) for source in range(lax.axis_size(axis))]
    return lax.ppermute(value, axis, pairs)


def span_copies(info_ref, local_any, other_any, sk_sc, sv_sc, sems, block, span):
    copies = []
    for j in range(local_any.shape[0]):
        for parity, source in ((0, local_any), (1, other_any)):
            slot = 2 * j + parity
            offset = pl.multiple_of(info_ref[2 + GROUP_DEVS + slot], span)
            for part, target in ((0, sk_sc), (1, sv_sc)):
                copies.append(
                    pltpu.make_async_copy(
                        source.at[j, pl.ds(2 * block + part * span, span), :],
                        target.at[pl.ds(offset, span), :],
                        sems.at[2 * slot + part],
                    )
                )
    return copies


def attn_kernel(plan, offset, first, final, info_ref, q_ref, *refs):
    refs = list(refs)
    n_arrays = max(array for array, _ in plan) + 1
    state_in = [] if first else [refs.pop(0) for _ in range(3)]
    kv_refs = [(refs.pop(0), refs.pop(0)) for _ in range(n_arrays)]
    if final:
        la_ref, oa_ref, o_ref = refs.pop(0), refs.pop(0), refs.pop(0)
        m_sc, l_sc, acc_sc, sk_sc, sv_sc, sems = refs
    else:
        m_out, l_out, acc_out, m_sc, l_sc, acc_sc = refs
    step = pl.program_id(0)
    last = pl.num_programs(0) - 1
    rows = q_ref.shape[0]
    block = kv_refs[0][0].shape[0]
    length = info_ref[0]
    first_token = info_ref[1]

    @pl.when(step == 0)
    def _init():
        if final:
            span = sk_sc.shape[0] // GROUP_DEVS
            for copy in span_copies(info_ref, la_ref, oa_ref, sk_sc, sv_sc, sems, block, span):
                copy.start()
        if first:
            m_sc[...] = jnp.full(m_sc.shape, NEG_FILL, jnp.float32)
            l_sc[...] = jnp.zeros(l_sc.shape, jnp.float32)
            acc_sc[...] = jnp.zeros(acc_sc.shape, jnp.float32)
        else:
            m_sc[...] = state_in[0][...]
            l_sc[...] = state_in[1][...]
            acc_sc[...] = state_in[2][...]

    def process(keys, values, allowed):
        s = lax.dot_general(
            q_ref[...], keys, (((1,), (1,)), ((), ())), preferred_element_type=jnp.float32
        )
        if allowed is not None:
            s = jnp.where(allowed, s, NEG_FILL)
        m_prev = m_sc[...]
        m_new = jnp.maximum(m_prev, jnp.max(s, axis=1, keepdims=True))
        alpha = jnp.exp2((m_prev - m_new) * EXP2_SCALE)
        p = jnp.exp2((s - m_new) * EXP2_SCALE)
        l_sc[...] = alpha * l_sc[...] + jnp.sum(p, axis=1, keepdims=True)
        pv = jnp.dot(p.astype(jnp.bfloat16), values, preferred_element_type=jnp.float32)
        acc_sc[...] = alpha * acc_sc[...] + pv
        m_sc[...] = m_new

    def slot(k_ref, v_ref, start):
        full = start + block <= length
        partial = jnp.logical_and(start < length, jnp.logical_not(full))

        @pl.when(full)
        def _():
            process(k_ref[...], v_ref[...], None)

        @pl.when(partial)
        def _():
            key_rows = start + lax.broadcasted_iota(jnp.int32, (rows, block), 1)
            process(k_ref[...], v_ref[...], key_rows < length)

    for array in range(n_arrays):
        steps = [i for i, (a, _) in enumerate(plan) if a == array]
        uses = functools.reduce(jnp.logical_or, [step == i for i in steps])

        @pl.when(uses)
        def _():
            slot(kv_refs[array][0], kv_refs[array][1], info_ref[2 + 2 * GROUP_DEVS + offset + step])

    if final:
        tokens = o_ref.shape[0]
        heads = rows // tokens

        @pl.when(step == last)
        def _span():
            span = sk_sc.shape[0] // GROUP_DEVS
            for copy in span_copies(info_ref, la_ref, oa_ref, sk_sc, sv_sc, sems, block, span):
                copy.wait()
            span_rows = sk_sc.shape[0]
            key_pos = lax.broadcasted_iota(jnp.int32, (rows, span_rows), 1)
            query_pos = first_token + lax.rem(
                lax.broadcasted_iota(jnp.int32, (rows, span_rows), 0), tokens
            )
            process(sk_sc[...], sv_sc[...], key_pos <= query_pos)
            for h in range(heads):
                rows_h = slice(h * tokens, (h + 1) * tokens)
                o_ref[:, h * HEAD_SIZE:(h + 1) * HEAD_SIZE] = (
                    acc_sc[rows_h, :] / l_sc[rows_h, :]
                ).astype(o_ref.dtype)
    else:
        @pl.when(step == last)
        def _save():
            m_out[...] = m_sc[...]
            l_out[...] = l_sc[...]
            acc_out[...] = acc_sc[...]


def index_map(plan, array):
    used = [(i, index) for i, (a, index) in enumerate(plan) if a == array]
    table = []
    for i in range(len(plan) + 1):
        before = [index for j, index in used if j <= i]
        table.append(before[-1] if before else used[0][1])

    def pick(k):
        result = table[-1]
        for i in reversed(range(len(table) - 1)):
            result = jnp.where(k == i, table[i], result)
        return result

    return pick


def attention(info, offset, q_rows, arrays, plan, state, span_sources, tokens, block, span):
    rows = q_rows.shape[0]
    first = state is None
    final = span_sources is not None
    n_steps = len(plan) + (1 if final else 0)
    fixed = lambda k, info: (0, 0)
    in_specs = [pl.BlockSpec((rows, HEAD_SIZE), fixed)]
    operands = [info, q_rows]
    if not first:
        in_specs += [pl.BlockSpec((rows, 1), fixed), pl.BlockSpec((rows, 1), fixed),
                     pl.BlockSpec((rows, HEAD_SIZE), fixed)]
        operands += list(state)
    for array_id, array in enumerate(arrays):
        pick = index_map(plan, array_id)
        in_specs += [
            pl.BlockSpec((None, block, HEAD_SIZE), lambda k, info, pick=pick: (pick(k), 0, 0)),
            pl.BlockSpec((None, block, HEAD_SIZE), lambda k, info, pick=pick: (pick(k), 1, 0)),
        ]
        operands += [array, array]
    scratch = [
        pltpu.VMEM((rows, 1), jnp.float32),
        pltpu.VMEM((rows, 1), jnp.float32),
        pltpu.VMEM((rows, HEAD_SIZE), jnp.float32),
    ]
    if final:
        in_specs += [pl.BlockSpec(memory_space=pl.ANY), pl.BlockSpec(memory_space=pl.ANY)]
        operands += list(span_sources)
        heads = rows // tokens
        out_shape = jax.ShapeDtypeStruct((tokens, heads * HEAD_SIZE), jnp.bfloat16)
        out_specs = pl.BlockSpec((tokens, heads * HEAD_SIZE), fixed)
        scratch += [
            pltpu.VMEM((GROUP_DEVS * span, HEAD_SIZE), jnp.bfloat16),
            pltpu.VMEM((GROUP_DEVS * span, HEAD_SIZE), jnp.bfloat16),
            pltpu.SemaphoreType.DMA((4 * GROUP_DEVS,)),
        ]
    else:
        out_shape = (
            jax.ShapeDtypeStruct((rows, 1), jnp.float32),
            jax.ShapeDtypeStruct((rows, 1), jnp.float32),
            jax.ShapeDtypeStruct((rows, HEAD_SIZE), jnp.float32),
        )
        out_specs = (pl.BlockSpec((rows, 1), fixed), pl.BlockSpec((rows, 1), fixed),
                     pl.BlockSpec((rows, HEAD_SIZE), fixed))
    flops = 4 * rows * block * HEAD_SIZE * n_steps
    return pl.pallas_call(
        functools.partial(attn_kernel, plan, offset, first, final),
        out_shape=out_shape,
        grid_spec=pltpu.PrefetchScalarGridSpec(
            num_scalar_prefetch=1,
            grid=(n_steps,),
            in_specs=in_specs,
            out_specs=out_specs,
            scratch_shapes=scratch,
        ),
        compiler_params=pltpu.CompilerParams(
            dimension_semantics=("arbitrary",), vmem_limit_bytes=56 * 1024 * 1024
        ),
        cost_estimate=pl.CostEstimate(
            flops=flops, transcendentals=rows * block * n_steps,
            bytes_accessed=n_steps * 2 * block * HEAD_SIZE * 2,
        ),
    )(*operands)


def pack_kernel(k_ref, v_ref, sk_ref, sv_ref, o_ref):
    rows = k_ref.shape[0]
    span = sk_ref.shape[0]
    o_ref[0:rows, :] = k_ref[...]
    o_ref[rows:2 * rows, :] = v_ref[...]
    o_ref[2 * rows:2 * rows + span, :] = sk_ref[...]
    o_ref[2 * rows + span:2 * rows + 2 * span, :] = sv_ref[...]


def make_pack(cache_k, cache_v, span_k, span_v):
    rows = 2 * cache_k.shape[0] + 2 * span_k.shape[0]
    return pl.pallas_call(
        pack_kernel,
        out_shape=jax.ShapeDtypeStruct((rows, HEAD_SIZE), cache_k.dtype),
    )(cache_k, cache_v, span_k, span_v)


def heads_as_rows(queries):
    tokens, width = queries.shape
    heads = width // HEAD_SIZE
    return queries.reshape(tokens, heads, HEAD_SIZE).transpose(1, 0, 2).reshape(heads * tokens, HEAD_SIZE)


def body(queries, span_rotated_keys, span_token_values, cache_keys, prompt_cache_values, lengths):
    tok_rows = queries.shape[0]
    cache_rows = cache_keys.shape[0]
    group_devs = lax.axis_size("req") // lengths.shape[0]
    assert group_devs == GROUP_DEVS
    device = lax.axis_index("req")
    position = device % GROUP_DEVS
    group_length = lax.dynamic_index_in_dim(lengths, device // GROUP_DEVS, 0, keepdims=False)

    pack = make_pack(cache_keys, prompt_cache_values, span_rotated_keys, span_token_values)
    span_rows = span_rotated_keys.shape[0]
    slot_pos = jnp.arange(GROUP_DEVS, dtype=jnp.int32) ^ position
    step_pos = jnp.asarray(STEP_SLOTS, jnp.int32) ^ position
    info = jnp.concatenate(
        [
            jnp.stack([group_length, position * tok_rows]).astype(jnp.int32),
            (slot_pos * cache_rows).astype(jnp.int32),
            (slot_pos * span_rows).astype(jnp.int32),
            (step_pos * cache_rows).astype(jnp.int32),
        ]
    )
    q_rows = heads_as_rows(queries)
    size = (tok_rows, cache_rows, span_rows)

    half = pack.shape[0] // 2
    from_x = exchange(pack, "req", 2)
    from_z = exchange(pack, "req", 4)
    state = attention(info, 0, q_rows, [pack[None]], [(0, 0)], None, None, *size)
    diag_lo = exchange(from_z[:half], "req", 2)
    diag_hi = exchange(from_x[half:], "req", 4)
    state = attention(
        info, 1, q_rows, [from_x[None], from_z[None]], [(0, 0), (1, 0)], state, None, *size
    )
    diag = jnp.concatenate([diag_lo, diag_hi], 0)
    local = jnp.stack([pack, from_x, from_z, diag])
    other = exchange(local, "req", 1)
    plan = [(0, 3), (1, 0), (1, 1), (1, 2), (1, 3)]
    attended = attention(info, 3, q_rows, [local, other], plan, state, (local, other), *size)
    hi, lo = lax.axis_size("tph"), lax.axis_size("tpl")
    pieces = attended.reshape(hi, lo, tok_rows // (hi * lo), attended.shape[1])
    pieces = lax.all_to_all(pieces.transpose(1, 0, 2, 3), "tpl", 0, 0)
    pieces = lax.all_to_all(pieces.transpose(1, 0, 2, 3), "tph", 0, 0)
    return pieces.transpose(2, 0, 1, 3).reshape(pieces.shape[2], -1)


def solution(mesh):
    tp_hi = TP_HI
    devices = mesh.devices.reshape(mesh.shape["req"], tp_hi, mesh.shape["tp"] // tp_hi)
    mesh = Mesh(devices, ("req", "tph", "tpl"))
    rows = P("req", ("tph", "tpl"))
    in_specs = (rows, rows, rows, rows, rows, P())
    out_specs = P(("req", "tph", "tpl"), None)
    return jax.shard_map(body, mesh=mesh, in_specs=in_specs, out_specs=out_specs, check_vma=False)
```

```python
import functools
import math

import jax
import jax.numpy as jnp
from jax import lax
from jax.experimental import pallas as pl
from jax.experimental.pallas import tpu as pltpu
from jax.sharding import PartitionSpec as P


HEAD_SIZE = 128
GROUP_DEVS = 8
STEP_SLOTS = (0, 2, 4, 6, 1, 3, 5, 7)
NEG_FILL = -1e30
SCALE = 1.0 / math.sqrt(HEAD_SIZE)
EXP2_SCALE = SCALE * math.log2(math.e)


def exchange(value, axis, mask):
    pairs = [(source, source ^ mask) for source in range(lax.axis_size(axis))]
    return lax.ppermute(value, axis, pairs)


def span_copies(info_ref, local_any, other_any, sk_sc, sv_sc, sems, block, span):
    copies = []
    for j in range(local_any.shape[0]):
        for parity, source in ((0, local_any), (1, other_any)):
            slot = 2 * j + parity
            offset = pl.multiple_of(info_ref[2 + GROUP_DEVS + slot], span)
            for part, target in ((0, sk_sc), (1, sv_sc)):
                copies.append(
                    pltpu.make_async_copy(
                        source.at[j, pl.ds(2 * block + part * span, span), :],
                        target.at[pl.ds(offset, span), :],
                        sems.at[2 * slot + part],
                    )
                )
    return copies


def attn_kernel(plan, offset, first, final, info_ref, q_ref, *refs):
    refs = list(refs)
    n_arrays = max(array for array, _ in plan) + 1
    state_in = [] if first else [refs.pop(0) for _ in range(3)]
    kv_refs = [(refs.pop(0), refs.pop(0)) for _ in range(n_arrays)]
    if final:
        la_ref, oa_ref, o_ref = refs.pop(0), refs.pop(0), refs.pop(0)
        m_sc, l_sc, acc_sc, sk_sc, sv_sc, sems = refs
    else:
        m_out, l_out, acc_out, m_sc, l_sc, acc_sc = refs
    step = pl.program_id(0)
    last = pl.num_programs(0) - 1
    rows = q_ref.shape[0]
    block = kv_refs[0][0].shape[0]
    length = info_ref[0]
    first_token = info_ref[1]

    @pl.when(step == 0)
    def _init():
        if final:
            span = sk_sc.shape[0] // GROUP_DEVS
            for copy in span_copies(info_ref, la_ref, oa_ref, sk_sc, sv_sc, sems, block, span):
                copy.start()
        if first:
            m_sc[...] = jnp.full(m_sc.shape, NEG_FILL, jnp.float32)
            l_sc[...] = jnp.zeros(l_sc.shape, jnp.float32)
            acc_sc[...] = jnp.zeros(acc_sc.shape, jnp.float32)
        else:
            m_sc[...] = state_in[0][...]
            l_sc[...] = state_in[1][...]
            acc_sc[...] = state_in[2][...]

    def process(keys, values, allowed):
        s = lax.dot_general(
            q_ref[...], keys, (((1,), (1,)), ((), ())), preferred_element_type=jnp.float32
        )
        if allowed is not None:
            s = jnp.where(allowed, s, NEG_FILL)
        m_prev = m_sc[...]
        m_new = jnp.maximum(m_prev, jnp.max(s, axis=1, keepdims=True))
        alpha = jnp.exp2((m_prev - m_new) * EXP2_SCALE)
        p = jnp.exp2((s - m_new) * EXP2_SCALE)
        l_sc[...] = alpha * l_sc[...] + jnp.sum(p, axis=1, keepdims=True)
        pv = jnp.dot(p.astype(jnp.bfloat16), values, preferred_element_type=jnp.float32)
        acc_sc[...] = alpha * acc_sc[...] + pv
        m_sc[...] = m_new

    def slot(k_ref, v_ref, start):
        full = start + block <= length
        partial = jnp.logical_and(start < length, jnp.logical_not(full))

        @pl.when(full)
        def _():
            process(k_ref[...], v_ref[...], None)

        @pl.when(partial)
        def _():
            key_rows = start + lax.broadcasted_iota(jnp.int32, (rows, block), 1)
            process(k_ref[...], v_ref[...], key_rows < length)

    for array in range(n_arrays):
        steps = [i for i, (a, _) in enumerate(plan) if a == array]
        uses = functools.reduce(jnp.logical_or, [step == i for i in steps])

        @pl.when(uses)
        def _():
            slot(kv_refs[array][0], kv_refs[array][1], info_ref[2 + 2 * GROUP_DEVS + offset + step])

    if final:
        tokens = o_ref.shape[0]
        heads = rows // tokens

        @pl.when(step == last)
        def _span():
            span = sk_sc.shape[0] // GROUP_DEVS
            for copy in span_copies(info_ref, la_ref, oa_ref, sk_sc, sv_sc, sems, block, span):
                copy.wait()
            span_rows = sk_sc.shape[0]
            key_pos = lax.broadcasted_iota(jnp.int32, (rows, span_rows), 1)
            query_pos = first_token + lax.rem(
                lax.broadcasted_iota(jnp.int32, (rows, span_rows), 0), tokens
            )
            process(sk_sc[...], sv_sc[...], key_pos <= query_pos)
            for h in range(heads):
                rows_h = slice(h * tokens, (h + 1) * tokens)
                o_ref[:, h * HEAD_SIZE:(h + 1) * HEAD_SIZE] = (
                    acc_sc[rows_h, :] / l_sc[rows_h, :]
                ).astype(o_ref.dtype)
    else:
        @pl.when(step == last)
        def _save():
            m_out[...] = m_sc[...]
            l_out[...] = l_sc[...]
            acc_out[...] = acc_sc[...]


def index_map(plan, array):
    used = [(i, index) for i, (a, index) in enumerate(plan) if a == array]
    table = []
    for i in range(len(plan) + 1):
        before = [index for j, index in used if j <= i]
        table.append(before[-1] if before else used[0][1])

    def pick(k):
        result = table[-1]
        for i in reversed(range(len(table) - 1)):
            result = jnp.where(k == i, table[i], result)
        return result

    return pick


def attention(info, offset, q_rows, arrays, plan, state, span_sources, tokens, block, span):
    rows = q_rows.shape[0]
    first = state is None
    final = span_sources is not None
    n_steps = len(plan) + (1 if final else 0)
    fixed = lambda k, info: (0, 0)
    in_specs = [pl.BlockSpec((rows, HEAD_SIZE), fixed)]
    operands = [info, q_rows]
    if not first:
        in_specs += [pl.BlockSpec((rows, 1), fixed), pl.BlockSpec((rows, 1), fixed),
                     pl.BlockSpec((rows, HEAD_SIZE), fixed)]
        operands += list(state)
    for array_id, array in enumerate(arrays):
        pick = index_map(plan, array_id)
        in_specs += [
            pl.BlockSpec((None, block, HEAD_SIZE), lambda k, info, pick=pick: (pick(k), 0, 0)),
            pl.BlockSpec((None, block, HEAD_SIZE), lambda k, info, pick=pick: (pick(k), 1, 0)),
        ]
        operands += [array, array]
    scratch = [
        pltpu.VMEM((rows, 1), jnp.float32),
        pltpu.VMEM((rows, 1), jnp.float32),
        pltpu.VMEM((rows, HEAD_SIZE), jnp.float32),
    ]
    if final:
        in_specs += [pl.BlockSpec(memory_space=pl.ANY), pl.BlockSpec(memory_space=pl.ANY)]
        operands += list(span_sources)
        heads = rows // tokens
        out_shape = jax.ShapeDtypeStruct((tokens, heads * HEAD_SIZE), jnp.bfloat16)
        out_specs = pl.BlockSpec((tokens, heads * HEAD_SIZE), fixed)
        scratch += [
            pltpu.VMEM((GROUP_DEVS * span, HEAD_SIZE), jnp.bfloat16),
            pltpu.VMEM((GROUP_DEVS * span, HEAD_SIZE), jnp.bfloat16),
            pltpu.SemaphoreType.DMA((4 * GROUP_DEVS,)),
        ]
    else:
        out_shape = (
            jax.ShapeDtypeStruct((rows, 1), jnp.float32),
            jax.ShapeDtypeStruct((rows, 1), jnp.float32),
            jax.ShapeDtypeStruct((rows, HEAD_SIZE), jnp.float32),
        )
        out_specs = (pl.BlockSpec((rows, 1), fixed), pl.BlockSpec((rows, 1), fixed),
                     pl.BlockSpec((rows, HEAD_SIZE), fixed))
    flops = 4 * rows * block * HEAD_SIZE * n_steps
    return pl.pallas_call(
        functools.partial(attn_kernel, plan, offset, first, final),
        out_shape=out_shape,
        grid_spec=pltpu.PrefetchScalarGridSpec(
            num_scalar_prefetch=1,
            grid=(n_steps,),
            in_specs=in_specs,
            out_specs=out_specs,
            scratch_shapes=scratch,
        ),
        compiler_params=pltpu.CompilerParams(
            dimension_semantics=("arbitrary",), vmem_limit_bytes=32 * 1024 * 1024
        ),
        cost_estimate=pl.CostEstimate(
            flops=flops, transcendentals=rows * block * n_steps,
            bytes_accessed=n_steps * 2 * block * HEAD_SIZE * 2,
        ),
    )(*operands)


def pack_kernel(k_ref, v_ref, sk_ref, sv_ref, o_ref):
    rows = k_ref.shape[0]
    span = sk_ref.shape[0]
    o_ref[0:rows, :] = k_ref[...]
    o_ref[rows:2 * rows, :] = v_ref[...]
    o_ref[2 * rows:2 * rows + span, :] = sk_ref[...]
    o_ref[2 * rows + span:2 * rows + 2 * span, :] = sv_ref[...]


def make_pack(cache_k, cache_v, span_k, span_v):
    rows = 2 * cache_k.shape[0] + 2 * span_k.shape[0]
    return pl.pallas_call(
        pack_kernel,
        out_shape=jax.ShapeDtypeStruct((rows, HEAD_SIZE), cache_k.dtype),
    )(cache_k, cache_v, span_k, span_v)


def heads_as_rows(queries):
    tokens, width = queries.shape
    heads = width // HEAD_SIZE
    return queries.reshape(tokens, heads, HEAD_SIZE).transpose(1, 0, 2).reshape(heads * tokens, HEAD_SIZE)


def body(queries, span_rotated_keys, span_token_values, cache_keys, prompt_cache_values, lengths):
    tok_rows = queries.shape[0]
    cache_rows = cache_keys.shape[0]
    group_devs = lax.axis_size("req") // lengths.shape[0]
    assert group_devs == GROUP_DEVS
    device = lax.axis_index("req")
    position = device % GROUP_DEVS
    group_length = lax.dynamic_index_in_dim(lengths, device // GROUP_DEVS, 0, keepdims=False)

    pack = make_pack(cache_keys, prompt_cache_values, span_rotated_keys, span_token_values)
    span_rows = span_rotated_keys.shape[0]
    slot_pos = jnp.arange(GROUP_DEVS, dtype=jnp.int32) ^ position
    step_pos = jnp.asarray(STEP_SLOTS, jnp.int32) ^ position
    info = jnp.concatenate(
        [
            jnp.stack([group_length, position * tok_rows]).astype(jnp.int32),
            (slot_pos * cache_rows).astype(jnp.int32),
            (slot_pos * span_rows).astype(jnp.int32),
            (step_pos * cache_rows).astype(jnp.int32),
        ]
    )
    q_rows = heads_as_rows(queries)
    size = (tok_rows, cache_rows, span_rows)

    half = pack.shape[0] // 2
    from_x = exchange(pack, "req", 2)
    from_z = exchange(pack, "req", 4)
    state = attention(info, 0, q_rows, [pack[None]], [(0, 0)], None, None, *size)
    diag_lo = exchange(from_z[:half], "req", 2)
    diag_hi = exchange(from_x[half:], "req", 4)
    state = attention(
        info, 1, q_rows, [from_x[None], from_z[None]], [(0, 0), (1, 0)], state, None, *size
    )
    diag = jnp.concatenate([diag_lo, diag_hi], 0)
    local = jnp.stack([pack, from_x, from_z, diag])
    other = exchange(local, "req", 1)
    state = attention(info, 3, q_rows, [local], [(0, 3)], state, None, *size)
    plan = [(0, 0), (0, 1), (0, 2), (0, 3)]
    attended = attention(info, 4, q_rows, [other], plan, state, (local, other), *size)
    return lax.all_to_all(attended, "tp", split_axis=0, concat_axis=1, tiled=True)


def solution(mesh):
    in_specs = (P("req", "tp"), P("req", "tp"), P("req", "tp"), P("req", "tp"), P("req", "tp"), P())
    out_specs = P(("req", "tp"), None)
    return jax.shard_map(body, mesh=mesh, in_specs=in_specs, out_specs=out_specs, check_vma=False)
```
